128 devices in a mesh: section: 2 (over z_lo), cp: 16 (over y, z_hi, core), tp: 4 (over x).
Axes of the slice: x: 4, y: 4, z: 4 (z_hi: 2, z_lo: 2; z = z_hi * 2 + z_lo), core: 2. Of those that a mesh axis runs over, the one named last changes fastest.
Arguments:
- rollout_rows: bfloat16 [2048, 8192], P(('section', 'cp'), 'tp'), may hold values from -60 to 60
- lengths: int32 [2], replicated, may hold values from 1 to 1536, 2048 in all
- block_owner: int32 [32], replicated, may hold values from 0 to 31, each once
- norm_gain: float32 [2, 8192], P('section', 'tp'), may hold values from 0.1 to 1.9
- w_qkv: bfloat16 [2, 3, 8192, 8192], P('section', None, 'tp', 'cp'), may hold values from -1 to 1
- w_out: bfloat16 [2, 8192, 8192], P('section', 'cp', 'tp'), may hold values from -0.5 to 0.5
Outputs:
- scored: bfloat16 [2, 2048, 8192], P(None, ('section', 'cp'), 'tp')
The draws below stay inside these ranges and needn't reach their ends.
Inputs may be any that keep to these rules, and one draw needn't show every extreme that they name: The 2 lengths sum to 2048; neither is over 1536. `block_owner`: every owner block appears once.
All inputs are finite; a program needn't handle non-finite values.
Results may differ from the reference program's by a relative error of at most 0.022.
Values may be sent and summed in bfloat16 or wider, within the bound.
No kernel may reach another device: no remote copies, remote signals or barrier semaphores. Data moves between devices by JAX's collectives and lax.ppermute only.
A program may use at most 128 MiB of HBM per device.

```python
import math
import jax
import jax.numpy as jnp
import numpy as np
from jax import lax

D = 8192
HEADS = 64
HEAD = 128
NSEQ = 2
TOKENS = 2048
MOST = 1536
NBLK = 32
N_CP = 16


def draw_rollout_rows(key, part):
    first, second, third = jax.random.split(key, 3)
    row_scale = jnp.exp(jax.random.uniform(first, (TOKENS, 1), jnp.float32, math.log(0.3), math.log(3.0)))
    column_ramp = jnp.arange(D, dtype=jnp.float32) / D - 0.5
    column_scale = jnp.power(10.0, column_ramp) * jnp.exp(jax.random.uniform(second, (D,), jnp.float32, -0.35, 0.35))
    entries = jax.random.truncated_normal(third, -4.0, 4.0, (TOKENS, D), jnp.float32)
    return (entries * row_scale * column_scale[None, :]).astype(jnp.bfloat16)


def draw_w_qkv(key, part):
    first = jax.random.fold_in(key, 0)
    entries = jax.random.truncated_normal(first, -4.0, 4.0, (2, 3, D, HEADS, HEAD), jnp.float32) / math.sqrt(D)
    return entries.reshape(2, 3, D, HEADS * HEAD).astype(jnp.bfloat16)


def block_scale(rng, shape, cuts, low, high):
    factor_of, own = 1.0, jax.random.fold_in(rng, 6)
    for axis_at, parts in cuts:
        heights = jnp.exp(jax.random.uniform(jax.random.fold_in(own, axis_at), (parts,), jnp.float32, low / len(cuts), high / len(cuts)))
        factor_of = factor_of * jnp.repeat(heights, shape[axis_at] // parts).reshape([-1 if axis == axis_at else 1 for axis in range(len(shape))])
    return factor_of


def length_profile(number_of, total, limit, skew):
    weights = [(1 << 20) // math.isqrt(standing ** skew) + 1 for standing in range(2, number_of + 1)]
    spare, given = total - limit - (number_of - 1), [1] * (number_of - 1)
    while spare > 0:
        candidates = [i for i in range(number_of - 1) if given[i] < limit]
        whole, remaining = sum([weights[i] for i in candidates]), spare
        for i in candidates:
            extra = min(limit - given[i], max(1, remaining * weights[i] // whole), spare)
            given[i] = given[i] + extra
            spare = spare - extra
    return np.array([limit] + given)


def uneven_parts(rng, amount, total, bound, skew):
    if amount == 2:
        one = jax.random.randint(rng, (), max(1, total - bound), min(bound, total - 1) + 1)
        return jnp.stack([one, total - one])
    tallies = jnp.asarray(length_profile(amount, total, bound, skew), jnp.int32)
    twos = (amount - 1) // 2
    donor, receiver = tallies[1:1 + 2 * twos:2], tallies[2:2 + 2 * twos:2]
    room = jnp.minimum(donor - 1, bound - receiver)
    moved = jax.random.randint(jax.random.fold_in(rng, 1), (twos,), 0, 1 << 20) % (room + 1)
    tallies = tallies.at[1:1 + 2 * twos:2].set(donor - moved).at[2:2 + 2 * twos:2].set(receiver + moved)
    return tallies[jax.random.permutation(jax.random.fold_in(rng, 2), amount)]


def scatter_about(own_key, extent, width, reach, pieces=(), kind=jnp.bfloat16):
    drawn = width * jax.random.normal(own_key, extent, jnp.float32)
    if pieces:
        drawn = drawn * block_scale(own_key, extent, pieces, -0.22, 0.18)
    return jnp.clip(drawn, -reach, reach).astype(kind)


def setup_inputs(seed: int = 0) -> dict:
    streams_of = jax.random.split(jax.random.key(seed), 7)
    return {
        "rollout_rows": draw_rollout_rows(jax.random.fold_in(streams_of[6], 71), 0),
        "lengths": uneven_parts(streams_of[1], NSEQ, TOKENS, MOST, 2).astype(jnp.int32),
        "block_owner": jax.random.permutation(streams_of[2], NBLK).astype(jnp.int32),
        "norm_gain": jnp.clip(1.0 + 0.18 * jax.random.normal(streams_of[3], (2, D), jnp.float32), 0.1, 1.9),
        "w_qkv": draw_w_qkv(jax.random.fold_in(streams_of[6], 71), 0),
        "w_out": scatter_about(streams_of[5], (2, HEADS * HEAD, D), HEAD ** -0.5, 0.5, ((0, 2), (1, 16), (2, 4))),
    }


def reference(rollout_rows, lengths, block_owner, norm_gain, w_qkv, w_out):
    own_rows = TOKENS // NBLK
    packed = rollout_rows.reshape(NBLK, own_rows, D)[block_owner].reshape(TOKENS, D)
    position = jnp.arange(TOKENS, dtype=jnp.int32)
    seq_ends = jnp.cumsum(lengths).astype(jnp.int32)
    sequence = lax.optimization_barrier(jnp.sum((position[:, None] >= seq_ends[None, :]).astype(jnp.int32), axis=1))
    allowed = (sequence[:, None] == sequence[None, :]) & (position[None, :] <= position[:, None])
    mean_square = lax.optimization_barrier(jnp.mean(jnp.square(packed.astype(jnp.float32)), axis=1, keepdims=True))
    inverse_rms = lax.rsqrt(mean_square + 1e-05)
    group_width = HEADS * HEAD // N_CP
    outputs = []
    for model_index in range(2):
        normed = (packed.astype(jnp.float32) * norm_gain[model_index][None, :] * inverse_rms).astype(jnp.bfloat16)
        projected = []
        for kind_index in range(3):
            result = jnp.dot(normed, w_qkv[model_index, kind_index], preferred_element_type=jnp.float32).astype(jnp.bfloat16)
            projected.append(result.reshape(TOKENS, HEADS, HEAD).transpose(1, 0, 2))

        def one_head(operands):
            queries, key_rows, value_rows = operands
            scores = jnp.dot(queries, key_rows.T, preferred_element_type=jnp.float32) / math.sqrt(HEAD)
            scores = jnp.where(allowed, scores, -1e+30)
            row_peak = lax.optimization_barrier(jnp.max(scores, axis=1, keepdims=True))
            weights = jnp.where(allowed, jnp.exp(scores - row_peak), 0.0)
            row_total = lax.optimization_barrier(jnp.sum(weights, axis=1, keepdims=True))
            probabilities = weights.astype(jnp.bfloat16)
            mixed = jnp.dot(probabilities, value_rows, preferred_element_type=jnp.float32)
            return (mixed / row_total).astype(jnp.bfloat16)
        attended = lax.map(one_head, (projected[0], projected[1], projected[2]))
        attended = attended.transpose(1, 0, 2).reshape(TOKENS, HEADS * HEAD)
        out_weight = w_out[model_index]

        def add_group(group_index, running):
            first_col = (group_index * group_width).astype(jnp.int32)
            columns = lax.dynamic_slice_in_dim(attended, first_col, group_width, 1)
            rows_of = lax.dynamic_slice_in_dim(out_weight, first_col, group_width, 0)
            partial_sum = jnp.dot(columns, rows_of, preferred_element_type=jnp.float32).astype(jnp.bfloat16)
            partial_sum = lax.optimization_barrier(partial_sum)
            return running + partial_sum.astype(jnp.float32)
        branch = lax.fori_loop(0, N_CP, add_group, jnp.zeros((TOKENS, D), jnp.float32)).astype(jnp.bfloat16)
        scored = jnp.zeros((NBLK, own_rows, D), jnp.bfloat16).at[block_owner].set(branch.reshape(NBLK, own_rows, D))
        outputs.append(scored.reshape(TOKENS, D))
    return jnp.stack(outputs)
```

```python
import math

import jax
import jax.numpy as jnp
from jax import lax
from jax.sharding import PartitionSpec as P

D = 8192
HEAD = 128


def on_device(rollout_rows, lengths, block_owner, norm_gain, w_qkv, w_out):
    tp_count = lax.axis_size("tp")
    cp_count = lax.axis_size("cp")
    sections = lax.axis_size("section")
    own_rows, width_here = rollout_rows.shape
    blocks = sections * cp_count
    tokens = own_rows * blocks

    rows_in = lax.all_gather(rollout_rows, ("cp", "section"), axis=0, tiled=True)
    layout_rows = jnp.arange(tokens, dtype=jnp.int32)
    cp_of = layout_rows // (sections * own_rows)
    section_of = layout_rows // own_rows % sections
    actor_block = section_of * cp_count + cp_of
    block_ids = jnp.arange(blocks, dtype=jnp.int32)
    packed_block = jnp.sum(
        jnp.where(block_owner[None, :] == block_ids[:, None], block_ids[None, :], 0), axis=1
    )
    position = packed_block[actor_block] * own_rows + layout_rows % own_rows
    seq_ends = jnp.cumsum(lengths)
    sequence = jnp.sum((position[:, None] >= seq_ends[None, :]).astype(jnp.int32), axis=1)

    rows_f32 = rows_in.astype(jnp.float32)
    squares = jnp.sum(jnp.square(rows_f32), axis=1)
    total_squares = lax.psum(squares, "tp")
    inverse_rms = lax.rsqrt(total_squares / D + 1e-05)
    scaled = (rows_f32 * norm_gain[0][None, :]).astype(jnp.bfloat16)

    qkv_weights = w_qkv[0]
    group_cols = qkv_weights.shape[2]
    heads_here = group_cols // HEAD
    weights4 = qkv_weights.reshape(3, width_here, heads_here, HEAD)
    partial = jnp.einsum(
        "rd,kdje->jrke", scaled, weights4, preferred_element_type=jnp.float32
    ).astype(jnp.bfloat16)
    partial = partial.reshape(heads_here * tokens, 3 * HEAD)
    one_head = lax.psum_scatter(partial, "tp", scatter_dimension=0, tiled=True)
    one_head = one_head.reshape(tokens, 3, HEAD)
    one_head = (one_head.astype(jnp.float32) * inverse_rms[:, None, None]).astype(jnp.bfloat16)
    queries = one_head[:, 0]
    key_rows = one_head[:, 1]
    value_rows = one_head[:, 2]

    allowed = (sequence[:, None] == sequence[None, :]) & (position[None, :] <= position[:, None])
    scores = jnp.dot(queries, key_rows.T, preferred_element_type=jnp.float32) / math.sqrt(HEAD)
    scores = jnp.where(allowed, scores, -1e30)
    row_peak = jnp.max(scores, axis=1, keepdims=True)
    weights = jnp.where(allowed, jnp.exp(scores - row_peak), 0.0)
    row_total = jnp.sum(weights, axis=1, keepdims=True)
    probabilities = weights.astype(jnp.bfloat16)
    mixed = jnp.dot(probabilities, value_rows, preferred_element_type=jnp.float32)
    attended = (mixed / row_total).astype(jnp.bfloat16)

    group_att = lax.all_gather(attended, "tp", axis=0, tiled=False)
    out_weight = w_out[0].reshape(tp_count, HEAD, width_here)
    partial_out = jnp.einsum(
        "jre,jew->rw", group_att, out_weight, preferred_element_type=jnp.float32
    ).astype(jnp.bfloat16)
    summed = lax.psum_scatter(partial_out, "cp", scatter_dimension=0, tiled=True)
    branch = summed.reshape(sections, own_rows, width_here)
    return lax.all_to_all(branch, "section", split_axis=0, concat_axis=0, tiled=True)


def solution(mesh):
    return jax.shard_map(
        on_device,
        mesh=mesh,
        in_specs=(
            P(("section", "cp"), "tp"),
            P(),
            P(),
            P("section", "tp"),
            P("section", None, "tp", "cp"),
            P("section", "cp", "tp"),
        ),
        out_specs=P(None, ("section", "cp"), "tp"),
        check_vma=False,
    )
```

```python
import math

import jax
import jax.numpy as jnp
from jax import lax
from jax.sharding import PartitionSpec as P

D = 8192
HEAD = 128


def on_device(rollout_rows, lengths, block_owner, norm_gain, w_qkv, w_out):
    tp_count = lax.axis_size("tp")
    cp_count = lax.axis_size("cp")
    sections = lax.axis_size("section")
    own_rows, width_here = rollout_rows.shape
    blocks = sections * cp_count
    tokens = own_rows * blocks

    rows_in = lax.all_gather(rollout_rows, ("section", "cp"), axis=0, tiled=True)
    block_ids = jnp.arange(blocks, dtype=jnp.int32)
    packed_block = jnp.sum(
        jnp.where(block_owner[None, :] == block_ids[:, None], block_ids[None, :], 0), axis=1
    )
    inner = jnp.arange(own_rows, dtype=jnp.int32)
    position = (packed_block[:, None] * own_rows + inner[None, :]).reshape(tokens)
    query_position = (
        packed_block.reshape(sections, cp_count).T.reshape(blocks)[:, None] * own_rows
        + inner[None, :]
    ).reshape(tokens)
    seq_ends = jnp.cumsum(lengths)
    sequence = jnp.sum((position[:, None] >= seq_ends[None, :]).astype(jnp.int32), axis=1)
    query_sequence = jnp.sum(
        (query_position[:, None] >= seq_ends[None, :]).astype(jnp.int32), axis=1
    )

    rows_f32 = rows_in.astype(jnp.float32)
    squares = jnp.sum(jnp.square(rows_f32), axis=1)
    total_squares = lax.psum(squares, "tp")
    inverse_rms = lax.rsqrt(total_squares / D + 1e-05)
    scaled = (rows_f32 * norm_gain[0][None, :]).astype(jnp.bfloat16)

    qkv_weights = w_qkv[0]
    group_cols = qkv_weights.shape[2]
    heads_here = group_cols // HEAD
    partial = jnp.stack(
        [
            jnp.einsum(
                "rd,kde->kre",
                scaled,
                qkv_weights[:, :, j * HEAD : (j + 1) * HEAD],
                preferred_element_type=jnp.float32,
            ).astype(jnp.bfloat16)
            for j in range(heads_here)
        ]
    )
    partial = partial.reshape(heads_here * 3 * tokens, HEAD)
    one_head = lax.psum_scatter(partial, "tp", scatter_dimension=0, tiled=True)
    one_head = one_head.reshape(3, tokens, HEAD)
    one_head = (one_head.astype(jnp.float32) * inverse_rms[None, :, None]).astype(jnp.bfloat16)
    queries = (
        one_head[0]
        .reshape(sections, cp_count, own_rows, HEAD)
        .transpose(1, 0, 2, 3)
        .reshape(tokens, HEAD)
    )
    key_rows = one_head[1]
    value_rows = one_head[2]

    allowed = (query_sequence[:, None] == sequence[None, :]) & (
        position[None, :] <= query_position[:, None]
    )
    scores = jnp.dot(queries, key_rows.T, preferred_element_type=jnp.float32) / math.sqrt(HEAD)
    scores = jnp.where(allowed, scores, -1e30)
    row_peak = jnp.max(scores, axis=1, keepdims=True)
    weights = jnp.where(allowed, jnp.exp(scores - row_peak), 0.0)
    row_total = jnp.sum(weights, axis=1, keepdims=True)
    probabilities = weights.astype(jnp.bfloat16)
    mixed = jnp.dot(probabilities, value_rows, preferred_element_type=jnp.float32)
    attended = (mixed / row_total).astype(jnp.bfloat16)

    group_att = lax.all_gather(attended, "tp", axis=0, tiled=False)
    out_weight = w_out[0].reshape(tp_count, HEAD, width_here)
    partial_out = jnp.einsum(
        "jre,jew->rw", group_att, out_weight, preferred_element_type=jnp.float32
    ).astype(jnp.bfloat16)
    summed = lax.psum_scatter(partial_out, "cp", scatter_dimension=0, tiled=True)
    branch = summed.reshape(sections, own_rows, width_here)
    return lax.all_to_all(branch, "section", split_axis=0, concat_axis=0, tiled=True)


def solution(mesh):
    return jax.shard_map(
        on_device,
        mesh=mesh,
        in_specs=(
            P(("section", "cp"), "tp"),
            P(),
            P(),
            P("section", "tp"),
            P("section", None, "tp", "cp"),
            P("section", "cp", "tp"),
        ),
        out_specs=P(None, ("section", "cp"), "tp"),
        check_vma=False,
    )
```

```python
import math

import jax
import jax.numpy as jnp
from jax import lax
from jax.sharding import PartitionSpec as P

D = 8192
HEAD = 128


def shifted(value, axis, count, step):
    return lax.ppermute(value, axis, perm=[(j, (j + step) % count) for j in range(count)])


def on_device(rollout_rows, lengths, block_owner, norm_gain, w_qkv, w_out):
    tp_count = lax.axis_size("tp")
    cp_count = lax.axis_size("cp")
    sections = lax.axis_size("section")
    own_rows, width_here = rollout_rows.shape
    blocks = sections * cp_count
    half = own_rows // 2
    me_tp = lax.axis_index("tp")
    me_section = lax.axis_index("section")

    block_ids = jnp.arange(blocks, dtype=jnp.int32)
    packed_block = jnp.sum(
        jnp.where(block_owner[None, :] == block_ids[:, None], block_ids[None, :], 0), axis=1
    )
    seq_ends = jnp.cumsum(lengths)

    def sequence_of(position):
        return jnp.sum((position[:, None] >= seq_ends[None, :]).astype(jnp.int32), axis=1)

    gain = norm_gain[0]
    qkv_weights = w_qkv[0]
    heads_here = qkv_weights.shape[2] // HEAD

    def project(rows):
        rows_f32 = rows.astype(jnp.float32)
        squares = jnp.sum(jnp.square(rows_f32), axis=1)
        total_squares = squares
        for step in range(1, tp_count):
            total_squares = total_squares + shifted(squares, "tp", tp_count, step)
        inverse_rms = lax.rsqrt(total_squares / D + 1e-05)
        scaled = (rows_f32 * gain[None, :]).astype(jnp.bfloat16)
        stacked = jnp.stack(
            [
                jnp.einsum(
                    "rd,kde->kre",
                    scaled,
                    qkv_weights[:, :, j * HEAD : (j + 1) * HEAD],
                    preferred_element_type=jnp.float32,
                ).astype(jnp.bfloat16)
                for j in range(heads_here)
            ]
        )
        summed = jnp.take(stacked, me_tp, axis=0).astype(jnp.float32)
        for step in range(1, tp_count):
            piece = jnp.take(stacked, (me_tp + step) % tp_count, axis=0)
            summed = summed + shifted(piece, "tp", tp_count, step).astype(jnp.float32)
        return (summed * inverse_rms[None, :, None]).astype(jnp.bfloat16)

    rows_a = lax.all_gather(rollout_rows[:half], ("section", "cp"), axis=0, tiled=True)
    qkv_a = project(rows_a)
    rows_b = lax.all_gather(rollout_rows[half:], ("section", "cp"), axis=0, tiled=True)
    qkv_b = project(rows_b)

    key_rows = jnp.concatenate([qkv_a[1], qkv_b[1]], axis=0)
    value_rows = jnp.concatenate([qkv_a[2], qkv_b[2]], axis=0)
    half_rows = jnp.arange(blocks * half, dtype=jnp.int32)
    key_position_a = packed_block[half_rows // half] * own_rows + half_rows % half
    key_position = jnp.concatenate([key_position_a, key_position_a + half])
    key_sequence = sequence_of(key_position)

    out_weight = w_out[0].reshape(tp_count, HEAD, width_here)
    source_of = (me_tp - jnp.arange(tp_count, dtype=jnp.int32)) % tp_count
    out_weight = jnp.take(out_weight, source_of, axis=0)
    inner = jnp.arange(own_rows, dtype=jnp.int32)
    group_rows = cp_count * half

    def attend(target):
        first = target * group_rows
        query_a = lax.dynamic_slice_in_dim(qkv_a[0], first, group_rows, 0)
        query_b = lax.dynamic_slice_in_dim(qkv_b[0], first, group_rows, 0)
        queries = jnp.concatenate(
            [query_a.reshape(cp_count, half, HEAD), query_b.reshape(cp_count, half, HEAD)], axis=1
        ).reshape(cp_count * own_rows, HEAD)
        owners = lax.dynamic_slice_in_dim(packed_block, target * cp_count, cp_count, 0)
        query_position = (owners[:, None] * own_rows + inner[None, :]).reshape(-1)
        query_sequence = sequence_of(query_position)
        allowed = (query_sequence[:, None] == key_sequence[None, :]) & (
            key_position[None, :] <= query_position[:, None]
        )
        scores = jnp.dot(queries, key_rows.T, preferred_element_type=jnp.float32) / math.sqrt(HEAD)
        scores = jnp.where(allowed, scores, -1e30)
        row_peak = jnp.max(scores, axis=1, keepdims=True)
        weights = jnp.where(allowed, jnp.exp(scores - row_peak), 0.0)
        row_total = jnp.sum(weights, axis=1, keepdims=True)
        probabilities = weights.astype(jnp.bfloat16)
        mixed = jnp.dot(probabilities, value_rows, preferred_element_type=jnp.float32)
        attended = (mixed / row_total).astype(jnp.bfloat16)
        parts = [attended] + [
            shifted(attended, "tp", tp_count, step) for step in range(1, tp_count)
        ]
        partial_out = jnp.einsum(
            "kre,kew->rw", jnp.stack(parts), out_weight, preferred_element_type=jnp.float32
        ).astype(jnp.bfloat16)
        return lax.psum_scatter(partial_out, "cp", scatter_dimension=0, tiled=True)

    other = attend(1 - me_section)
    received = shifted(other, "section", sections, 1)
    own = attend(me_section)
    return jnp.where(me_section == 0, jnp.stack([own, received]), jnp.stack([received, own]))


def solution(mesh):
    return jax.shard_map(
        on_device,
        mesh=mesh,
        in_specs=(
            P(("section", "cp"), "tp"),
            P(),
            P(),
            P("section", "tp"),
            P("section", None, "tp", "cp"),
            P("section", "cp", "tp"),
        ),
        out_specs=P(None, ("section", "cp"), "tp"),
        check_vma=False,
    )
```

```python
import math

import jax
import jax.numpy as jnp
from jax import lax
from jax.sharding import PartitionSpec as P

D = 8192
HEAD = 128


def shifted(value, axis, count, step):
    return lax.ppermute(value, axis, perm=[(j, (j + step) % count) for j in range(count)])


def on_device(rollout_rows, lengths, block_owner, norm_gain, w_qkv, w_out):
    tp_count = lax.axis_size("tp")
    cp_count = lax.axis_size("cp")
    sections = lax.axis_size("section")
    own_rows, width_here = rollout_rows.shape
    blocks = sections * cp_count
    tokens = own_rows * blocks

    rows_in = lax.all_gather(rollout_rows, ("section", "cp"), axis=0, tiled=True)
    block_ids = jnp.arange(blocks, dtype=jnp.int32)
    packed_block = jnp.sum(
        jnp.where(block_owner[None, :] == block_ids[:, None], block_ids[None, :], 0), axis=1
    )
    inner = jnp.arange(own_rows, dtype=jnp.int32)
    position = (packed_block[:, None] * own_rows + inner[None, :]).reshape(tokens)
    query_position = (
        packed_block.reshape(sections, cp_count).T.reshape(blocks)[:, None] * own_rows
        + inner[None, :]
    ).reshape(tokens)
    seq_ends = jnp.cumsum(lengths)
    sequence = jnp.sum((position[:, None] >= seq_ends[None, :]).astype(jnp.int32), axis=1)
    query_sequence = jnp.sum(
        (query_position[:, None] >= seq_ends[None, :]).astype(jnp.int32), axis=1
    )

    me_tp = lax.axis_index("tp")
    rows_f32 = rows_in.astype(jnp.float32)
    squares = jnp.sum(jnp.square(rows_f32), axis=1)
    total_squares = squares
    for step in range(1, tp_count):
        total_squares = total_squares + shifted(squares, "tp", tp_count, step)
    inverse_rms = lax.rsqrt(total_squares / D + 1e-05)
    scaled = (rows_f32 * norm_gain[0][None, :]).astype(jnp.bfloat16)

    qkv_weights = w_qkv[0]

    def head_partial(head):
        head_weights = lax.dynamic_slice_in_dim(qkv_weights, head * HEAD, HEAD, axis=2)
        return jnp.einsum("rd,kde->kre", scaled, head_weights, preferred_element_type=jnp.float32)

    summed = head_partial(me_tp)
    for step in range(1, tp_count):
        piece = head_partial((me_tp + step) % tp_count).astype(jnp.bfloat16)
        summed = summed + shifted(piece, "tp", tp_count, step).astype(jnp.float32)
    one_head = (summed * inverse_rms[None, :, None]).astype(jnp.bfloat16)
    queries = (
        one_head[0]
        .reshape(sections, cp_count, own_rows, HEAD)
        .transpose(1, 0, 2, 3)
        .reshape(tokens, HEAD)
    )
    key_rows = one_head[1]
    value_rows = one_head[2]

    allowed = (query_sequence[:, None] == sequence[None, :]) & (
        position[None, :] <= query_position[:, None]
    )
    scores = jnp.dot(queries, key_rows.T, preferred_element_type=jnp.float32) / math.sqrt(HEAD)
    scores = jnp.where(allowed, scores, -1e30)
    row_peak = jnp.max(scores, axis=1, keepdims=True)
    weights = jnp.where(allowed, jnp.exp(scores - row_peak), 0.0)
    row_total = jnp.sum(weights, axis=1, keepdims=True)
    probabilities = weights.astype(jnp.bfloat16)
    mixed = jnp.dot(probabilities, value_rows, preferred_element_type=jnp.float32)
    attended = (mixed / row_total).astype(jnp.bfloat16)

    parts = [attended] + [shifted(attended, "tp", tp_count, step) for step in range(1, tp_count)]
    out_weight = w_out[0].reshape(tp_count, HEAD, width_here)
    source_of = (me_tp - jnp.arange(tp_count, dtype=jnp.int32)) % tp_count
    out_weight = jnp.take(out_weight, source_of, axis=0)
    partial_out = jnp.einsum(
        "kre,kew->rw", jnp.stack(parts), out_weight, preferred_element_type=jnp.float32
    ).astype(jnp.bfloat16)
    reduced = lax.psum_scatter(partial_out, "cp", scatter_dimension=0, tiled=True)
    branch = reduced.reshape(sections, own_rows, width_here)
    return lax.all_to_all(branch, "section", split_axis=0, concat_axis=0, tiled=True)


def solution(mesh):
    return jax.shard_map(
        on_device,
        mesh=mesh,
        in_specs=(
            P(("section", "cp"), "tp"),
            P(),
            P(),
            P("section", "tp"),
            P("section", None, "tp", "cp"),
            P("section", "cp", "tp"),
        ),
        out_specs=P(None, ("section", "cp"), "tp"),
        check_vma=False,
    )
```

```python
import math

import jax
import jax.numpy as jnp
from jax import lax
from jax.sharding import PartitionSpec as P

D = 8192
HEAD = 128


def shifted(value, axis, count, step):
    return lax.ppermute(value, axis, perm=[(j, (j + step) % count) for j in range(count)])


def on_device(rollout_rows, lengths, block_owner, norm_gain, w_qkv, w_out):
    tp_count = lax.axis_size("tp")
    cp_count = lax.axis_size("cp")
    sections = lax.axis_size("section")
    own_rows, width_here = rollout_rows.shape
    blocks = sections * cp_count
    tokens = own_rows * blocks

    rows_in = lax.all_gather(rollout_rows, ("section", "cp"), axis=0, tiled=True)
    block_ids = jnp.arange(blocks, dtype=jnp.int32)
    packed_block = jnp.sum(
        jnp.where(block_owner[None, :] == block_ids[:, None], block_ids[None, :], 0), axis=1
    )
    inner = jnp.arange(own_rows, dtype=jnp.int32)
    position = (packed_block[:, None] * own_rows + inner[None, :]).reshape(tokens)
    y_count = cp_count // 4
    query_order = (
        packed_block.reshape(sections, y_count, 2, 2).transpose(3, 1, 2, 0).reshape(blocks)
    )
    query_position = (query_order[:, None] * own_rows + inner[None, :]).reshape(tokens)
    seq_ends = jnp.cumsum(lengths)
    sequence = jnp.sum((position[:, None] >= seq_ends[None, :]).astype(jnp.int32), axis=1)
    query_sequence = jnp.sum(
        (query_position[:, None] >= seq_ends[None, :]).astype(jnp.int32), axis=1
    )

    me_tp = lax.axis_index("tp")
    rows_f32 = rows_in.astype(jnp.float32)
    squares = jnp.sum(jnp.square(rows_f32), axis=1)
    total_squares = squares
    for step in range(1, tp_count):
        total_squares = total_squares + shifted(squares, "tp", tp_count, step)
    inverse_rms = lax.rsqrt(total_squares / D + 1e-05)
    scaled = (rows_f32 * norm_gain[0][None, :]).astype(jnp.bfloat16)

    qkv_weights = w_qkv[0]

    def head_partial(head):
        head_weights = lax.dynamic_slice_in_dim(qkv_weights, head * HEAD, HEAD, axis=2)
        return jnp.einsum("rd,kde->kre", scaled, head_weights, preferred_element_type=jnp.float32)

    summed = head_partial(me_tp)
    for step in range(1, tp_count):
        piece = head_partial((me_tp + step) % tp_count).astype(jnp.bfloat16)
        summed = summed + shifted(piece, "tp", tp_count, step).astype(jnp.float32)
    one_head = (summed * inverse_rms[None, :, None]).astype(jnp.bfloat16)
    queries = (
        one_head[0]
        .reshape(sections, y_count, 2, 2, own_rows, HEAD)
        .transpose(3, 1, 2, 0, 4, 5)
        .reshape(tokens, HEAD)
    )
    key_rows = one_head[1]
    value_rows = one_head[2]

    allowed = (query_sequence[:, None] == sequence[None, :]) & (
        position[None, :] <= query_position[:, None]
    )
    scores = jnp.dot(queries, key_rows.T, preferred_element_type=jnp.float32) / math.sqrt(HEAD)
    scores = jnp.where(allowed, scores, -1e30)
    row_peak = jnp.max(scores, axis=1, keepdims=True)
    weights = jnp.where(allowed, jnp.exp(scores - row_peak), 0.0)
    row_total = jnp.sum(weights, axis=1, keepdims=True)
    probabilities = weights.astype(jnp.bfloat16)
    mixed = jnp.dot(probabilities, value_rows, preferred_element_type=jnp.float32)
    attended = (mixed / row_total).astype(jnp.bfloat16)

    parts = [attended] + [shifted(attended, "tp", tp_count, step) for step in range(1, tp_count)]
    out_weight = w_out[0].reshape(tp_count, HEAD, width_here)
    source_of = (me_tp - jnp.arange(tp_count, dtype=jnp.int32)) % tp_count
    out_weight = jnp.take(out_weight, source_of, axis=0)
    partial_out = jnp.einsum(
        "kre,kew->rw", jnp.stack(parts), out_weight, preferred_element_type=jnp.float32
    ).astype(jnp.bfloat16)
    me_cp = lax.axis_index("cp")
    me_section = lax.axis_index("section")
    me_core = me_cp % 2
    me_y = me_cp // 4
    me_z = me_cp // 2 % 2
    staged = partial_out.reshape(2, y_count, 2, sections, own_rows, width_here)
    kept = lax.dynamic_index_in_dim(staged, me_core, 0, keepdims=False)
    given = lax.dynamic_index_in_dim(staged, 1 - me_core, 0, keepdims=False)
    core_perm = [(c, c ^ 1) for c in range(cp_count)]
    chip_sum = kept.astype(jnp.float32) + lax.ppermute(given, "cp", core_perm).astype(jnp.float32)
    chip_half = chip_sum.astype(jnp.bfloat16)
    y_sum = lax.dynamic_index_in_dim(chip_sum, me_y, 0, keepdims=False)
    for step in range(1, y_count):
        piece = lax.dynamic_index_in_dim(chip_half, (me_y + step) % y_count, 0, keepdims=False)
        y_perm = [(c, ((c // 4 + step) % y_count) * 4 + c % 4) for c in range(cp_count)]
        y_sum = y_sum + lax.ppermute(piece, "cp", y_perm).astype(jnp.float32)
    y_half = y_sum.astype(jnp.bfloat16)

    def piece_of(z_index, section_index):
        z_part = lax.dynamic_index_in_dim(y_half, z_index, 0, keepdims=False)
        return lax.dynamic_index_in_dim(z_part, section_index, 0, keepdims=False)

    flat = sections * cp_count
    z_flip = [(g, g // cp_count * cp_count + (g % cp_count ^ 2)) for g in range(flat)]
    s_flip = [(g, (g + cp_count) % flat) for g in range(flat)]
    both_flip = [(g, (g + cp_count) % flat // cp_count * cp_count + (g % cp_count ^ 2)) for g in range(flat)]
    axes = ("section", "cp")
    own_total = lax.dynamic_index_in_dim(
        lax.dynamic_index_in_dim(y_sum, me_z, 0, keepdims=False), me_section, 0, keepdims=False
    ) + lax.ppermute(piece_of(1 - me_z, me_section), axes, z_flip).astype(jnp.float32)
    other_total = lax.ppermute(piece_of(me_z, 1 - me_section), axes, s_flip).astype(
        jnp.float32
    ) + lax.ppermute(piece_of(1 - me_z, 1 - me_section), axes, both_flip).astype(jnp.float32)
    own_total = own_total.astype(jnp.bfloat16)
    other_total = other_total.astype(jnp.bfloat16)
    return jnp.where(
        me_section == 0, jnp.stack([own_total, other_total]), jnp.stack([other_total, own_total])
    )

def solution(mesh):
    return jax.shard_map(
        on_device,
        mesh=mesh,
        in_specs=(
            P(("section", "cp"), "tp"),
            P(),
            P(),
            P("section", "tp"),
            P("section", None, "tp", "cp"),
            P("section", "cp", "tp"),
        ),
        out_specs=P(None, ("section", "cp"), "tp"),
        check_vma=False,
    )
```

```python
import math

import jax
import jax.numpy as jnp
from jax import lax
from jax.sharding import PartitionSpec as P

D = 8192
HEAD = 128


def shifted(value, axis, count, step):
    return lax.ppermute(value, axis, perm=[(j, (j + step) % count) for j in range(count)])


def on_device(rollout_rows, lengths, block_owner, norm_gain, w_qkv, w_out):
    tp_count = lax.axis_size("tp")
    cp_count = lax.axis_size("cp")
    sections = lax.axis_size("section")
    own_rows, width_here = rollout_rows.shape
    blocks = sections * cp_count
    tokens = own_rows * blocks

    rows_in = lax.all_gather(rollout_rows, ("section", "cp"), axis=0, tiled=True)
    block_ids = jnp.arange(blocks, dtype=jnp.int32)
    packed_block = jnp.sum(
        jnp.where(block_owner[None, :] == block_ids[:, None], block_ids[None, :], 0), axis=1
    )
    inner = jnp.arange(own_rows, dtype=jnp.int32)
    position = (packed_block[:, None] * own_rows + inner[None, :]).reshape(tokens)
    y_count = cp_count // 4
    query_order = (
        packed_block.reshape(sections, y_count, 2, 2).transpose(3, 1, 2, 0).reshape(blocks)
    )
    query_position = (query_order[:, None] * own_rows + inner[None, :]).reshape(tokens)
    seq_ends = jnp.cumsum(lengths)
    sequence = jnp.sum((position[:, None] >= seq_ends[None, :]).astype(jnp.int32), axis=1)
    query_sequence = jnp.sum(
        (query_position[:, None] >= seq_ends[None, :]).astype(jnp.int32), axis=1
    )

    me_tp = lax.axis_index("tp")
    rows_f32 = rows_in.astype(jnp.float32)
    squares = jnp.sum(jnp.square(rows_f32), axis=1)
    total_squares = squares
    for step in range(1, tp_count):
        total_squares = total_squares + shifted(squares, "tp", tp_count, step)
    inverse_rms = lax.rsqrt(total_squares / D + 1e-05)
    scaled = (rows_f32 * norm_gain[0][None, :]).astype(jnp.bfloat16)

    qkv_weights = w_qkv[0]

    def head_partial(head):
        head_weights = lax.dynamic_slice_in_dim(qkv_weights, head * HEAD, HEAD, axis=2)
        return jnp.einsum("rd,kde->kre", scaled, head_weights, preferred_element_type=jnp.float32)

    summed = head_partial(me_tp)
    for step in range(1, tp_count):
        piece = head_partial((me_tp + step) % tp_count).astype(jnp.bfloat16)
        summed = summed + shifted(piece, "tp", tp_count, step).astype(jnp.float32)
    one_head = (summed * inverse_rms[None, :, None]).astype(jnp.bfloat16)
    queries = (
        one_head[0]
        .reshape(sections, y_count, 2, 2, own_rows, HEAD)
        .transpose(3, 1, 2, 0, 4, 5)
        .reshape(tokens, HEAD)
    )
    key_rows = one_head[1]
    value_rows = one_head[2]

    me_cp = lax.axis_index("cp")
    me_section = lax.axis_index("section")
    me_core = me_cp % 2
    me_y = me_cp // 4
    me_z = me_cp // 2 % 2
    out_weight = w_out[0].reshape(tp_count, HEAD, width_here)
    source_of = (me_tp - jnp.arange(tp_count, dtype=jnp.int32)) % tp_count
    out_weight = jnp.take(out_weight, source_of, axis=0)
    flat = sections * cp_count
    z_flip = [(g, g // cp_count * cp_count + (g % cp_count ^ 2)) for g in range(flat)]
    s_flip = [(g, (g + cp_count) % flat) for g in range(flat)]
    both_flip = [
        (g, (g + cp_count) % flat // cp_count * cp_count + (g % cp_count ^ 2)) for g in range(flat)
    ]
    axes = ("section", "cp")
    core_perm = [(c, c ^ 1) for c in range(cp_count)]

    def back_half(chunk_queries, chunk_position, chunk_sequence):
        chunk_rows = chunk_queries.shape[0] // blocks
        allowed = (chunk_sequence[:, None] == sequence[None, :]) & (
            position[None, :] <= chunk_position[:, None]
        )
        scores = jnp.dot(chunk_queries, key_rows.T, preferred_element_type=jnp.float32)
        scores = jnp.where(allowed, scores / math.sqrt(HEAD), -1e30)
        row_peak = jnp.max(scores, axis=1, keepdims=True)
        weights = jnp.where(allowed, jnp.exp(scores - row_peak), 0.0)
        row_total = jnp.sum(weights, axis=1, keepdims=True)
        probabilities = weights.astype(jnp.bfloat16)
        mixed = jnp.dot(probabilities, value_rows, preferred_element_type=jnp.float32)
        attended = (mixed / row_total).astype(jnp.bfloat16)
        parts = [attended] + [
            shifted(attended, "tp", tp_count, step) for step in range(1, tp_count)
        ]
        partial_out = jnp.einsum(
            "kre,kew->rw", jnp.stack(parts), out_weight, preferred_element_type=jnp.float32
        ).astype(jnp.bfloat16)
        staged = partial_out.reshape(2, y_count, 2, sections, chunk_rows, width_here)
        kept = lax.dynamic_index_in_dim(staged, me_core, 0, keepdims=False)
        given = lax.dynamic_index_in_dim(staged, 1 - me_core, 0, keepdims=False)
        chip_sum = kept.astype(jnp.float32) + lax.ppermute(given, "cp", core_perm).astype(
            jnp.float32
        )
        chip_half = chip_sum.astype(jnp.bfloat16)
        y_sum = lax.dynamic_index_in_dim(chip_sum, me_y, 0, keepdims=False)
        for step in range(1, y_count):
            piece = lax.dynamic_index_in_dim(
                chip_half, (me_y + step) % y_count, 0, keepdims=False
            )
            y_perm = [(c, ((c // 4 + step) % y_count) * 4 + c % 4) for c in range(cp_count)]
            y_sum = y_sum + lax.ppermute(piece, "cp", y_perm).astype(jnp.float32)
        y_half = y_sum.astype(jnp.bfloat16)

        def piece_of(z_index, section_index):
            z_part = lax.dynamic_index_in_dim(y_half, z_index, 0, keepdims=False)
            return lax.dynamic_index_in_dim(z_part, section_index, 0, keepdims=False)

        own_part = lax.dynamic_index_in_dim(
            lax.dynamic_index_in_dim(y_sum, me_z, 0, keepdims=False), me_section, 0, keepdims=False
        )
        own_total = own_part + lax.ppermute(piece_of(1 - me_z, me_section), axes, z_flip).astype(
            jnp.float32
        )
        other_total = lax.ppermute(piece_of(me_z, 1 - me_section), axes, s_flip).astype(
            jnp.float32
        ) + lax.ppermute(piece_of(1 - me_z, 1 - me_section), axes, both_flip).astype(jnp.float32)
        return own_total.astype(jnp.bfloat16), other_total.astype(jnp.bfloat16)

    chunks = 2
    chunk_rows = own_rows // chunks
    query_blocks = queries.reshape(blocks, own_rows, HEAD)
    position_blocks = query_position.reshape(blocks, own_rows)
    sequence_blocks = query_sequence.reshape(blocks, own_rows)
    own_parts, other_parts = [], []
    for chunk in range(chunks):
        rows_of = slice(chunk * chunk_rows, (chunk + 1) * chunk_rows)
        own_part, other_part = back_half(
            query_blocks[:, rows_of].reshape(-1, HEAD),
            position_blocks[:, rows_of].reshape(-1),
            sequence_blocks[:, rows_of].reshape(-1),
        )
        own_parts.append(own_part)
        other_parts.append(other_part)
    own_total = jnp.concatenate(own_parts, axis=0)
    other_total = jnp.concatenate(other_parts, axis=0)
    return jnp.where(
        me_section == 0, jnp.stack([own_total, other_total]), jnp.stack([other_total, own_total])
    )

def solution(mesh):
    return jax.shard_map(
        on_device,
        mesh=mesh,
        in_specs=(
            P(("section", "cp"), "tp"),
            P(),
            P(),
            P("section", "tp"),
            P("section", None, "tp", "cp"),
            P("section", "cp", "tp"),
        ),
        out_specs=P(None, ("section", "cp"), "tp"),
        check_vma=False,
    )
```

```python
import math

import jax
import jax.numpy as jnp
from jax import lax
from jax.sharding import PartitionSpec as P

D = 8192
HEAD = 128


def shifted(value, axis, count, step):
    return lax.ppermute(value, axis, perm=[(j, (j + step) % count) for j in range(count)])


def on_device(rollout_rows, lengths, block_owner, norm_gain, w_qkv, w_out):
    tp_count = lax.axis_size("tp")
    cp_count = lax.axis_size("cp")
    sections = lax.axis_size("section")
    own_rows, width_here = rollout_rows.shape
    blocks = sections * cp_count
    tokens = own_rows * blocks

    y_count = cp_count // 4
    me_section = lax.axis_index("section")
    me_cp = lax.axis_index("cp")
    me_core = me_cp % 2
    me_y = me_cp // 4
    me_z = me_cp // 2 % 2
    me_ring = me_z * 2 + me_section
    flat = sections * cp_count
    axes = ("section", "cp")

    def coords(g):
        c = g % cp_count
        return g // cp_count, c // 4, c // 2 % 2, c % 2

    def linear(s_i, y_i, z_i, core_i):
        return s_i * cp_count + y_i * 4 + z_i * 2 + core_i

    def ring_perm(step):
        pairs = []
        for g in range(flat):
            s_i, y_i, z_i, core_i = coords(g)
            ring = (z_i * 2 + s_i + step) % 4
            pairs.append((g, linear(ring % 2, y_i, ring // 2, core_i)))
        return pairs

    def y_perm(step):
        pairs = []
        for g in range(flat):
            s_i, y_i, z_i, core_i = coords(g)
            pairs.append((g, linear(s_i, (y_i + step) % y_count, z_i, core_i)))
        return pairs

    pair_perm = [(g, g ^ 1) for g in range(flat)]

    def gather_rows(local):
        ring_parts = [local] + [lax.ppermute(local, axes, ring_perm(k)) for k in range(1, 4)]
        ring_stack = jnp.stack(ring_parts)
        y_parts = [ring_stack] + [
            lax.ppermute(ring_stack, axes, y_perm(k)) for k in range(1, y_count)
        ]
        y_stack = jnp.stack(y_parts)
        both = jnp.stack([y_stack, lax.ppermute(y_stack, axes, pair_perm)])
        return both.reshape(-1, local.shape[-1])

    kc = jnp.arange(2, dtype=jnp.int32)[:, None, None]
    ky = jnp.arange(y_count, dtype=jnp.int32)[None, :, None]
    kz = jnp.arange(4, dtype=jnp.int32)[None, None, :]
    src_ring = (me_ring - kz) % 4
    actor_of = (
        (src_ring % 2) * cp_count
        + ((me_y - ky) % y_count) * 4
        + (src_ring // 2) * 2
        + (me_core ^ kc)
    ).reshape(blocks)
    half = own_rows // 2
    rows_parts = [gather_rows(rollout_rows[:half]), gather_rows(rollout_rows[half:])]

    block_ids = jnp.arange(blocks, dtype=jnp.int32)
    packed_block = jnp.sum(
        jnp.where(block_owner[None, :] == block_ids[:, None], block_ids[None, :], 0), axis=1
    )
    inner = jnp.arange(own_rows, dtype=jnp.int32)
    half_inner = jnp.arange(half, dtype=jnp.int32)
    layout_start = packed_block[actor_of] * own_rows
    position = jnp.concatenate(
        [
            (layout_start[:, None] + half_inner[None, :]).reshape(-1),
            (layout_start[:, None] + half + half_inner[None, :]).reshape(-1),
        ]
    )
    query_order = (
        packed_block.reshape(sections, y_count, 2, 2).transpose(3, 1, 2, 0).reshape(blocks)
    )
    query_position = (query_order[:, None] * own_rows + inner[None, :]).reshape(tokens)
    seq_ends = jnp.cumsum(lengths)
    sequence = jnp.sum((position[:, None] >= seq_ends[None, :]).astype(jnp.int32), axis=1)
    query_sequence = jnp.sum(
        (query_position[:, None] >= seq_ends[None, :]).astype(jnp.int32), axis=1
    )

    me_tp = lax.axis_index("tp")
    qkv_weights = w_qkv[0]

    def project(rows_in):
        rows_f32 = rows_in.astype(jnp.float32)
        squares = jnp.sum(jnp.square(rows_f32), axis=1)
        total_squares = squares
        for step in range(1, tp_count):
            total_squares = total_squares + shifted(squares, "tp", tp_count, step)
        inverse_rms = lax.rsqrt(total_squares / D + 1e-05)
        scaled = (rows_f32 * norm_gain[0][None, :]).astype(jnp.bfloat16)

        def head_partial(head):
            head_weights = lax.dynamic_slice_in_dim(qkv_weights, head * HEAD, HEAD, axis=2)
            return jnp.einsum(
                "rd,kde->kre", scaled, head_weights, preferred_element_type=jnp.float32
            )

        summed = head_partial(me_tp)
        for step in range(1, tp_count):
            piece = head_partial((me_tp + step) % tp_count).astype(jnp.bfloat16)
            summed = summed + shifted(piece, "tp", tp_count, step).astype(jnp.float32)
        return (summed * inverse_rms[None, :, None]).astype(jnp.bfloat16)

    qkv_parts = [project(part) for part in rows_parts]
    key_rows = jnp.concatenate([part[1] for part in qkv_parts], axis=0)
    value_rows = jnp.concatenate([part[2] for part in qkv_parts], axis=0)
    t_core = jnp.arange(2, dtype=jnp.int32)[:, None, None, None]
    t_y = jnp.arange(y_count, dtype=jnp.int32)[None, :, None, None]
    t_z = jnp.arange(2, dtype=jnp.int32)[None, None, :, None]
    t_s = jnp.arange(sections, dtype=jnp.int32)[None, None, None, :]
    layout_of = (
        ((t_core ^ me_core) * y_count + (me_y - t_y) % y_count) * 4
        + (me_ring - (t_z * 2 + t_s)) % 4
    ).reshape(blocks)
    queries = jnp.concatenate(
        [jnp.take(part[0].reshape(blocks, half, HEAD), layout_of, axis=0) for part in qkv_parts],
        axis=1,
    ).reshape(tokens, HEAD)

    out_weight = w_out[0].reshape(tp_count, HEAD, width_here)
    source_of = (me_tp - jnp.arange(tp_count, dtype=jnp.int32)) % tp_count
    out_weight = jnp.take(out_weight, source_of, axis=0)
    z_flip = [(g, g // cp_count * cp_count + (g % cp_count ^ 2)) for g in range(flat)]
    s_flip = [(g, (g + cp_count) % flat) for g in range(flat)]
    both_flip = [
        (g, (g + cp_count) % flat // cp_count * cp_count + (g % cp_count ^ 2)) for g in range(flat)
    ]
    core_perm = [(c, c ^ 1) for c in range(cp_count)]

    def back_half(chunk_queries, chunk_position, chunk_sequence):
        chunk_rows = chunk_queries.shape[0] // blocks
        allowed = (chunk_sequence[:, None] == sequence[None, :]) & (
            position[None, :] <= chunk_position[:, None]
        )
        scores = jnp.dot(chunk_queries, key_rows.T, preferred_element_type=jnp.float32)
        scores = jnp.where(allowed, scores / math.sqrt(HEAD), -1e30)
        row_peak = jnp.max(scores, axis=1, keepdims=True)
        weights = jnp.where(allowed, jnp.exp(scores - row_peak), 0.0)
        row_total = jnp.sum(weights, axis=1, keepdims=True)
        probabilities = weights.astype(jnp.bfloat16)
        mixed = jnp.dot(probabilities, value_rows, preferred_element_type=jnp.float32)
        attended = (mixed / row_total).astype(jnp.bfloat16)
        parts = [attended] + [
            shifted(attended, "tp", tp_count, step) for step in range(1, tp_count)
        ]
        partial_out = jnp.einsum(
            "kre,kew->rw", jnp.stack(parts), out_weight, preferred_element_type=jnp.float32
        ).astype(jnp.bfloat16)
        staged = partial_out.reshape(2, y_count, 2, sections, chunk_rows, width_here)
        kept = lax.dynamic_index_in_dim(staged, me_core, 0, keepdims=False)
        given = lax.dynamic_index_in_dim(staged, 1 - me_core, 0, keepdims=False)
        chip_sum = kept.astype(jnp.float32) + lax.ppermute(given, "cp", core_perm).astype(
            jnp.float32
        )
        chip_half = chip_sum.astype(jnp.bfloat16)
        y_sum = lax.dynamic_index_in_dim(chip_sum, me_y, 0, keepdims=False)
        for step in range(1, y_count):
            piece = lax.dynamic_index_in_dim(
                chip_half, (me_y + step) % y_count, 0, keepdims=False
            )
            y_perm = [(c, ((c // 4 + step) % y_count) * 4 + c % 4) for c in range(cp_count)]
            y_sum = y_sum + lax.ppermute(piece, "cp", y_perm).astype(jnp.float32)
        y_half = y_sum.astype(jnp.bfloat16)

        def piece_of(z_index, section_index):
            z_part = lax.dynamic_index_in_dim(y_half, z_index, 0, keepdims=False)
            return lax.dynamic_index_in_dim(z_part, section_index, 0, keepdims=False)

        own_part = lax.dynamic_index_in_dim(
            lax.dynamic_index_in_dim(y_sum, me_z, 0, keepdims=False), me_section, 0, keepdims=False
        )
        own_total = own_part + lax.ppermute(piece_of(1 - me_z, me_section), axes, z_flip).astype(
            jnp.float32
        )
        other_total = lax.ppermute(piece_of(me_z, 1 - me_section), axes, s_flip).astype(
            jnp.float32
        ) + lax.ppermute(piece_of(1 - me_z, 1 - me_section), axes, both_flip).astype(jnp.float32)
        return own_total.astype(jnp.bfloat16), other_total.astype(jnp.bfloat16)

    chunks = 2
    chunk_rows = own_rows // chunks
    query_blocks = queries.reshape(blocks, own_rows, HEAD)
    position_blocks = query_position.reshape(blocks, own_rows)
    sequence_blocks = query_sequence.reshape(blocks, own_rows)
    own_parts, other_parts = [], []
    for chunk in range(chunks):
        rows_of = slice(chunk * chunk_rows, (chunk + 1) * chunk_rows)
        own_part, other_part = back_half(
            query_blocks[:, rows_of].reshape(-1, HEAD),
            position_blocks[:, rows_of].reshape(-1),
            sequence_blocks[:, rows_of].reshape(-1),
        )
        own_parts.append(own_part)
        other_parts.append(other_part)
    own_total = jnp.concatenate(own_parts, axis=0)
    other_total = jnp.concatenate(other_parts, axis=0)
    return jnp.where(
        me_section == 0, jnp.stack([own_total, other_total]), jnp.stack([other_total, own_total])
    )

def solution(mesh):
    return jax.shard_map(
        on_device,
        mesh=mesh,
        in_specs=(
            P(("section", "cp"), "tp"),
            P(),
            P(),
            P("section", "tp"),
            P("section", None, "tp", "cp"),
            P("section", "cp", "tp"),
        ),
        out_specs=P(None, ("section", "cp"), "tp"),
        check_vma=False,
    )
```

```python
import math

import jax
import jax.numpy as jnp
from jax import lax
from jax.sharding import PartitionSpec as P

D = 8192
HEAD = 128


def shifted(value, axis, count, step):
    return lax.ppermute(value, axis, perm=[(j, (j + step) % count) for j in range(count)])


def on_device(rollout_rows, lengths, block_owner, norm_gain, w_qkv, w_out):
    tp_count = lax.axis_size("tp")
    cp_count = lax.axis_size("cp")
    sections = lax.axis_size("section")
    own_rows, width_here = rollout_rows.shape
    blocks = sections * cp_count
    tokens = own_rows * blocks

    y_count = cp_count // 4
    me_section = lax.axis_index("section")
    me_cp = lax.axis_index("cp")
    me_core = me_cp % 2
    me_y = me_cp // 4
    me_z = me_cp // 2 % 2
    me_ring = me_z * 2 + me_section
    flat = sections * cp_count
    axes = ("section", "cp")

    def coords(g):
        c = g % cp_count
        return g // cp_count, c // 4, c // 2 % 2, c % 2

    def linear(s_i, y_i, z_i, core_i):
        return s_i * cp_count + y_i * 4 + z_i * 2 + core_i

    def ring_perm(step):
        pairs = []
        for g in range(flat):
            s_i, y_i, z_i, core_i = coords(g)
            ring = (z_i * 2 + s_i + step) % 4
            pairs.append((g, linear(ring % 2, y_i, ring // 2, core_i)))
        return pairs

    def y_perm(step):
        pairs = []
        for g in range(flat):
            s_i, y_i, z_i, core_i = coords(g)
            pairs.append((g, linear(s_i, (y_i + step) % y_count, z_i, core_i)))
        return pairs

    pair_perm = [(g, g ^ 1) for g in range(flat)]

    def gather_rows(local):
        ring_parts = [local] + [lax.ppermute(local, axes, ring_perm(k)) for k in range(1, 4)]
        ring_stack = jnp.stack(ring_parts)
        y_parts = [ring_stack] + [
            lax.ppermute(ring_stack, axes, y_perm(k)) for k in range(1, y_count)
        ]
        y_stack = jnp.stack(y_parts)
        both = jnp.stack([y_stack, lax.ppermute(y_stack, axes, pair_perm)])
        return both.reshape(-1, local.shape[-1])

    kc = jnp.arange(2, dtype=jnp.int32)[:, None, None]
    ky = jnp.arange(y_count, dtype=jnp.int32)[None, :, None]
    kz = jnp.arange(4, dtype=jnp.int32)[None, None, :]
    src_ring = (me_ring - kz) % 4
    actor_of = (
        (src_ring % 2) * cp_count
        + ((me_y - ky) % y_count) * 4
        + (src_ring // 2) * 2
        + (me_core ^ kc)
    ).reshape(blocks)
    half = own_rows // 2
    first_rows = gather_rows(rollout_rows[:half])
    second_local, first_rows = lax.optimization_barrier((rollout_rows[half:], first_rows))
    rows_parts = [first_rows, gather_rows(second_local)]

    block_ids = jnp.arange(blocks, dtype=jnp.int32)
    packed_block = jnp.sum(
        jnp.where(block_owner[None, :] == block_ids[:, None], block_ids[None, :], 0), axis=1
    )
    inner = jnp.arange(own_rows, dtype=jnp.int32)
    half_inner = jnp.arange(half, dtype=jnp.int32)
    layout_start = packed_block[actor_of] * own_rows
    position = jnp.concatenate(
        [
            (layout_start[:, None] + half_inner[None, :]).reshape(-1),
            (layout_start[:, None] + half + half_inner[None, :]).reshape(-1),
        ]
    )
    query_order = (
        packed_block.reshape(sections, y_count, 2, 2).transpose(3, 1, 2, 0).reshape(blocks)
    )
    query_position = (query_order[:, None] * own_rows + inner[None, :]).reshape(tokens)
    seq_ends = jnp.cumsum(lengths)
    sequence = jnp.sum((position[:, None] >= seq_ends[None, :]).astype(jnp.int32), axis=1)
    query_sequence = jnp.sum(
        (query_position[:, None] >= seq_ends[None, :]).astype(jnp.int32), axis=1
    )

    me_tp = lax.axis_index("tp")
    qkv_weights = w_qkv[0]

    def project(rows_in):
        rows_f32 = rows_in.astype(jnp.float32)
        squares = jnp.sum(jnp.square(rows_f32), axis=1)
        total_squares = squares
        for step in range(1, tp_count):
            total_squares = total_squares + shifted(squares, "tp", tp_count, step)
        inverse_rms = lax.rsqrt(total_squares / D + 1e-05)
        scaled = (rows_f32 * norm_gain[0][None, :]).astype(jnp.bfloat16)

        def head_partial(head):
            head_weights = lax.dynamic_slice_in_dim(qkv_weights, head * HEAD, HEAD, axis=2)
            return jnp.einsum(
                "rd,kde->kre", scaled, head_weights, preferred_element_type=jnp.float32
            )

        summed = head_partial(me_tp)
        for step in range(1, tp_count):
            piece = head_partial((me_tp + step) % tp_count).astype(jnp.bfloat16)
            summed = summed + shifted(piece, "tp", tp_count, step).astype(jnp.float32)
        return (summed * inverse_rms[None, :, None]).astype(jnp.bfloat16)

    qkv_parts = [project(part) for part in rows_parts]
    key_rows = jnp.concatenate([part[1] for part in qkv_parts], axis=0)
    value_rows = jnp.concatenate([part[2] for part in qkv_parts], axis=0)
    t_core = jnp.arange(2, dtype=jnp.int32)[:, None, None, None]
    t_y = jnp.arange(y_count, dtype=jnp.int32)[None, :, None, None]
    t_z = jnp.arange(2, dtype=jnp.int32)[None, None, :, None]
    t_s = jnp.arange(sections, dtype=jnp.int32)[None, None, None, :]
    layout_of = (
        ((t_core ^ me_core) * y_count + (me_y - t_y) % y_count) * 4
        + (me_ring - (t_z * 2 + t_s)) % 4
    ).reshape(blocks)
    queries = jnp.concatenate(
        [jnp.take(part[0].reshape(blocks, half, HEAD), layout_of, axis=0) for part in qkv_parts],
        axis=1,
    ).reshape(tokens, HEAD)

    out_weight = w_out[0].reshape(tp_count, HEAD, width_here)
    source_of = (me_tp - jnp.arange(tp_count, dtype=jnp.int32)) % tp_count
    out_weight = jnp.take(out_weight, source_of, axis=0)
    z_flip = [(g, g // cp_count * cp_count + (g % cp_count ^ 2)) for g in range(flat)]
    s_flip = [(g, (g + cp_count) % flat) for g in range(flat)]
    both_flip = [
        (g, (g + cp_count) % flat // cp_count * cp_count + (g % cp_count ^ 2)) for g in range(flat)
    ]
    core_perm = [(c, c ^ 1) for c in range(cp_count)]

    def back_half(chunk_queries, chunk_position, chunk_sequence):
        chunk_rows = chunk_queries.shape[0] // blocks
        allowed = (chunk_sequence[:, None] == sequence[None, :]) & (
            position[None, :] <= chunk_position[:, None]
        )
        scores = jnp.dot(chunk_queries, key_rows.T, preferred_element_type=jnp.float32)
        scores = jnp.where(allowed, scores / math.sqrt(HEAD), -1e30)
        row_peak = jnp.max(scores, axis=1, keepdims=True)
        weights = jnp.where(allowed, jnp.exp(scores - row_peak), 0.0)
        row_total = jnp.sum(weights, axis=1, keepdims=True)
        probabilities = weights.astype(jnp.bfloat16)
        mixed = jnp.dot(probabilities, value_rows, preferred_element_type=jnp.float32)
        attended = (mixed / row_total).astype(jnp.bfloat16)
        parts = [attended] + [
            shifted(attended, "tp", tp_count, step) for step in range(1, tp_count)
        ]
        partial_out = jnp.einsum(
            "kre,kew->rw", jnp.stack(parts), out_weight, preferred_element_type=jnp.float32
        ).astype(jnp.bfloat16)
        staged = partial_out.reshape(2, y_count, 2, sections, chunk_rows, width_here)
        kept = lax.dynamic_index_in_dim(staged, me_core, 0, keepdims=False)
        given = lax.dynamic_index_in_dim(staged, 1 - me_core, 0, keepdims=False)
        chip_sum = kept.astype(jnp.float32) + lax.ppermute(given, "cp", core_perm).astype(
            jnp.float32
        )
        chip_half = chip_sum.astype(jnp.bfloat16)
        y_sum = lax.dynamic_index_in_dim(chip_sum, me_y, 0, keepdims=False)
        for step in range(1, y_count):
            piece = lax.dynamic_index_in_dim(
                chip_half, (me_y + step) % y_count, 0, keepdims=False
            )
            y_perm = [(c, ((c // 4 + step) % y_count) * 4 + c % 4) for c in range(cp_count)]
            y_sum = y_sum + lax.ppermute(piece, "cp", y_perm).astype(jnp.float32)
        y_half = y_sum.astype(jnp.bfloat16)

        def piece_of(z_index, section_index):
            z_part = lax.dynamic_index_in_dim(y_half, z_index, 0, keepdims=False)
            return lax.dynamic_index_in_dim(z_part, section_index, 0, keepdims=False)

        own_part = lax.dynamic_index_in_dim(
            lax.dynamic_index_in_dim(y_sum, me_z, 0, keepdims=False), me_section, 0, keepdims=False
        )
        own_total = own_part + lax.ppermute(piece_of(1 - me_z, me_section), axes, z_flip).astype(
            jnp.float32
        )
        other_total = lax.ppermute(piece_of(me_z, 1 - me_section), axes, s_flip).astype(
            jnp.float32
        ) + lax.ppermute(piece_of(1 - me_z, 1 - me_section), axes, both_flip).astype(jnp.float32)
        return own_total.astype(jnp.bfloat16), other_total.astype(jnp.bfloat16)

    chunks = 2
    chunk_rows = own_rows // chunks
    query_blocks = queries.reshape(blocks, own_rows, HEAD)
    position_blocks = query_position.reshape(blocks, own_rows)
    sequence_blocks = query_sequence.reshape(blocks, own_rows)
    own_parts, other_parts = [], []
    for chunk in range(chunks):
        rows_of = slice(chunk * chunk_rows, (chunk + 1) * chunk_rows)
        own_part, other_part = back_half(
            query_blocks[:, rows_of].reshape(-1, HEAD),
            position_blocks[:, rows_of].reshape(-1),
            sequence_blocks[:, rows_of].reshape(-1),
        )
        own_parts.append(own_part)
        other_parts.append(other_part)
    own_total = jnp.concatenate(own_parts, axis=0)
    other_total = jnp.concatenate(other_parts, axis=0)
    return jnp.where(
        me_section == 0, jnp.stack([own_total, other_total]), jnp.stack([other_total, own_total])
    )

def solution(mesh):
    return jax.shard_map(
        on_device,
        mesh=mesh,
        in_specs=(
            P(("section", "cp"), "tp"),
            P(),
            P(),
            P("section", "tp"),
            P("section", None, "tp", "cp"),
            P("section", "cp", "tp"),
        ),
        out_specs=P(None, ("section", "cp"), "tp"),
        check_vma=False,
    )
```

```python
import math

import jax
import jax.numpy as jnp
from jax import lax
from jax.sharding import PartitionSpec as P

D = 8192
HEAD = 128


def shifted(value, axis, count, step):
    return lax.ppermute(value, axis, perm=[(j, (j + step) % count) for j in range(count)])


def on_device(rollout_rows, lengths, block_owner, norm_gain, w_qkv, w_out):
    tp_count = lax.axis_size("tp")
    cp_count = lax.axis_size("cp")
    sections = lax.axis_size("section")
    own_rows, width_here = rollout_rows.shape
    blocks = sections * cp_count
    tokens = own_rows * blocks

    y_count = cp_count // 4
    me_section = lax.axis_index("section")
    me_cp = lax.axis_index("cp")
    me_core = me_cp % 2
    me_y = me_cp // 4
    me_z = me_cp // 2 % 2
    me_ring = me_z * 2 + me_section
    flat = sections * cp_count
    axes = ("section", "cp")

    def coords(g):
        c = g % cp_count
        return g // cp_count, c // 4, c // 2 % 2, c % 2

    def linear(s_i, y_i, z_i, core_i):
        return s_i * cp_count + y_i * 4 + z_i * 2 + core_i

    def ring_perm(step):
        pairs = []
        for g in range(flat):
            s_i, y_i, z_i, core_i = coords(g)
            ring = (z_i * 2 + s_i + step) % 4
            pairs.append((g, linear(ring % 2, y_i, ring // 2, core_i)))
        return pairs

    def y_perm(step):
        pairs = []
        for g in range(flat):
            s_i, y_i, z_i, core_i = coords(g)
            pairs.append((g, linear(s_i, (y_i + step) % y_count, z_i, core_i)))
        return pairs

    pair_perm = [(g, g ^ 1) for g in range(flat)]

    def gather_rows(local):
        ring_parts = [local] + [lax.ppermute(local, axes, ring_perm(k)) for k in range(1, 4)]
        ring_stack = jnp.stack(ring_parts)
        y_parts = [ring_stack] + [
            lax.ppermute(ring_stack, axes, y_perm(k)) for k in range(1, y_count)
        ]
        y_stack = jnp.stack(y_parts)
        both = jnp.stack([y_stack, lax.ppermute(y_stack, axes, pair_perm)])
        return both.reshape(-1, local.shape[-1])

    kc = jnp.arange(2, dtype=jnp.int32)[:, None, None]
    ky = jnp.arange(y_count, dtype=jnp.int32)[None, :, None]
    kz = jnp.arange(4, dtype=jnp.int32)[None, None, :]
    src_ring = (me_ring - kz) % 4
    actor_of = (
        (src_ring % 2) * cp_count
        + ((me_y - ky) % y_count) * 4
        + (src_ring // 2) * 2
        + (me_core ^ kc)
    ).reshape(blocks)
    half = own_rows // 2
    rows_parts = [gather_rows(rollout_rows[:half])]

    block_ids = jnp.arange(blocks, dtype=jnp.int32)
    packed_block = jnp.sum(
        jnp.where(block_owner[None, :] == block_ids[:, None], block_ids[None, :], 0), axis=1
    )
    inner = jnp.arange(own_rows, dtype=jnp.int32)
    half_inner = jnp.arange(half, dtype=jnp.int32)
    layout_start = packed_block[actor_of] * own_rows
    position = jnp.concatenate(
        [
            (layout_start[:, None] + half_inner[None, :]).reshape(-1),
            (layout_start[:, None] + half + half_inner[None, :]).reshape(-1),
        ]
    )
    query_order = (
        packed_block.reshape(sections, y_count, 2, 2).transpose(3, 1, 2, 0).reshape(blocks)
    )
    query_position = (query_order[:, None] * own_rows + inner[None, :]).reshape(tokens)
    seq_ends = jnp.cumsum(lengths)
    sequence = jnp.sum((position[:, None] >= seq_ends[None, :]).astype(jnp.int32), axis=1)
    query_sequence = jnp.sum(
        (query_position[:, None] >= seq_ends[None, :]).astype(jnp.int32), axis=1
    )

    me_tp = lax.axis_index("tp")
    qkv_weights = w_qkv[0]

    def partial_sums(rows_in):
        rows_f32 = rows_in.astype(jnp.float32)
        squares = jnp.sum(jnp.square(rows_f32), axis=1)
        scaled = (rows_f32 * norm_gain[0][None, :]).astype(jnp.bfloat16)

        def head_partial(head):
            head_weights = lax.dynamic_slice_in_dim(qkv_weights, head * HEAD, HEAD, axis=2)
            return jnp.einsum(
                "rd,kde->kre", scaled, head_weights, preferred_element_type=jnp.float32
            )

        own = head_partial(me_tp)
        pieces = [
            head_partial((me_tp + step) % tp_count).astype(jnp.bfloat16)
            for step in range(1, tp_count)
        ]
        return squares, own, pieces

    def reduce_heads(squares, own, pieces):
        total_squares = squares
        summed = own
        for step in range(1, tp_count):
            total_squares = total_squares + shifted(squares, "tp", tp_count, step)
            summed = summed + shifted(pieces[step - 1], "tp", tp_count, step).astype(jnp.float32)
        inverse_rms = lax.rsqrt(total_squares / D + 1e-05)
        return (summed * inverse_rms[None, :, None]).astype(jnp.bfloat16)

    first_sums = partial_sums(rows_parts[0])
    second_local, first_sums = lax.optimization_barrier((rollout_rows[half:], first_sums))
    qkv_parts = [reduce_heads(*first_sums)]
    qkv_parts.append(reduce_heads(*partial_sums(gather_rows(second_local))))
    key_rows = jnp.concatenate([part[1] for part in qkv_parts], axis=0)
    value_rows = jnp.concatenate([part[2] for part in qkv_parts], axis=0)
    t_core = jnp.arange(2, dtype=jnp.int32)[:, None, None, None]
    t_y = jnp.arange(y_count, dtype=jnp.int32)[None, :, None, None]
    t_z = jnp.arange(2, dtype=jnp.int32)[None, None, :, None]
    t_s = jnp.arange(sections, dtype=jnp.int32)[None, None, None, :]
    layout_of = (
        ((t_core ^ me_core) * y_count + (me_y - t_y) % y_count) * 4
        + (me_ring - (t_z * 2 + t_s)) % 4
    ).reshape(blocks)
    queries = jnp.concatenate(
        [jnp.take(part[0].reshape(blocks, half, HEAD), layout_of, axis=0) for part in qkv_parts],
        axis=1,
    ).reshape(tokens, HEAD)

    out_weight = w_out[0].reshape(tp_count, HEAD, width_here)
    source_of = (me_tp - jnp.arange(tp_count, dtype=jnp.int32)) % tp_count
    out_weight = jnp.take(out_weight, source_of, axis=0)
    z_flip = [(g, g // cp_count * cp_count + (g % cp_count ^ 2)) for g in range(flat)]
    s_flip = [(g, (g + cp_count) % flat) for g in range(flat)]
    both_flip = [
        (g, (g + cp_count) % flat // cp_count * cp_count + (g % cp_count ^ 2)) for g in range(flat)
    ]
    core_perm = [(c, c ^ 1) for c in range(cp_count)]

    def back_half(chunk_queries, chunk_position, chunk_sequence):
        chunk_rows = chunk_queries.shape[0] // blocks
        allowed = (chunk_sequence[:, None] == sequence[None, :]) & (
            position[None, :] <= chunk_position[:, None]
        )
        scores = jnp.dot(chunk_queries, key_rows.T, preferred_element_type=jnp.float32)
        scores = jnp.where(allowed, scores / math.sqrt(HEAD), -1e30)
        row_peak = jnp.max(scores, axis=1, keepdims=True)
        weights = jnp.where(allowed, jnp.exp(scores - row_peak), 0.0)
        row_total = jnp.sum(weights, axis=1, keepdims=True)
        probabilities = weights.astype(jnp.bfloat16)
        mixed = jnp.dot(probabilities, value_rows, preferred_element_type=jnp.float32)
        attended = (mixed / row_total).astype(jnp.bfloat16)
        parts = [attended] + [
            shifted(attended, "tp", tp_count, step) for step in range(1, tp_count)
        ]
        partial_out = jnp.einsum(
            "kre,kew->rw", jnp.stack(parts), out_weight, preferred_element_type=jnp.float32
        ).astype(jnp.bfloat16)
        staged = partial_out.reshape(2, y_count, 2, sections, chunk_rows, width_here)
        kept = lax.dynamic_index_in_dim(staged, me_core, 0, keepdims=False)
        given = lax.dynamic_index_in_dim(staged, 1 - me_core, 0, keepdims=False)
        chip_sum = kept.astype(jnp.float32) + lax.ppermute(given, "cp", core_perm).astype(
            jnp.float32
        )
        chip_half = chip_sum.astype(jnp.bfloat16)
        y_sum = lax.dynamic_index_in_dim(chip_sum, me_y, 0, keepdims=False)
        for step in range(1, y_count):
            piece = lax.dynamic_index_in_dim(
                chip_half, (me_y + step) % y_count, 0, keepdims=False
            )
            y_perm = [(c, ((c // 4 + step) % y_count) * 4 + c % 4) for c in range(cp_count)]
            y_sum = y_sum + lax.ppermute(piece, "cp", y_perm).astype(jnp.float32)
        y_half = y_sum.astype(jnp.bfloat16)

        def piece_of(z_index, section_index):
            z_part = lax.dynamic_index_in_dim(y_half, z_index, 0, keepdims=False)
            return lax.dynamic_index_in_dim(z_part, section_index, 0, keepdims=False)

        own_part = lax.dynamic_index_in_dim(
            lax.dynamic_index_in_dim(y_sum, me_z, 0, keepdims=False), me_section, 0, keepdims=False
        )
        own_total = own_part + lax.ppermute(piece_of(1 - me_z, me_section), axes, z_flip).astype(
            jnp.float32
        )
        other_total = lax.ppermute(piece_of(me_z, 1 - me_section), axes, s_flip).astype(
            jnp.float32
        ) + lax.ppermute(piece_of(1 - me_z, 1 - me_section), axes, both_flip).astype(jnp.float32)
        return own_total.astype(jnp.bfloat16), other_total.astype(jnp.bfloat16)

    chunks = 2
    chunk_rows = own_rows // chunks
    query_blocks = queries.reshape(blocks, own_rows, HEAD)
    position_blocks = query_position.reshape(blocks, own_rows)
    sequence_blocks = query_sequence.reshape(blocks, own_rows)
    own_parts, other_parts = [], []
    for chunk in range(chunks):
        rows_of = slice(chunk * chunk_rows, (chunk + 1) * chunk_rows)
        own_part, other_part = back_half(
            query_blocks[:, rows_of].reshape(-1, HEAD),
            position_blocks[:, rows_of].reshape(-1),
            sequence_blocks[:, rows_of].reshape(-1),
        )
        own_parts.append(own_part)
        other_parts.append(other_part)
    own_total = jnp.concatenate(own_parts, axis=0)
    other_total = jnp.concatenate(other_parts, axis=0)
    return jnp.where(
        me_section == 0, jnp.stack([own_total, other_total]), jnp.stack([other_total, own_total])
    )

def solution(mesh):
    return jax.shard_map(
        on_device,
        mesh=mesh,
        in_specs=(
            P(("section", "cp"), "tp"),
            P(),
            P(),
            P("section", "tp"),
            P("section", None, "tp", "cp"),
            P("section", "cp", "tp"),
        ),
        out_specs=P(None, ("section", "cp"), "tp"),
        check_vma=False,
    )
```

```python
import math

import jax
import jax.numpy as jnp
from jax import lax
from jax.sharding import PartitionSpec as P

D = 8192
HEAD = 128


def shifted(value, axis, count, step):
    return lax.ppermute(value, axis, perm=[(j, (j + step) % count) for j in range(count)])


def on_device(rollout_rows, lengths, block_owner, norm_gain, w_qkv, w_out):
    tp_count = lax.axis_size("tp")
    cp_count = lax.axis_size("cp")
    sections = lax.axis_size("section")
    own_rows, width_here = rollout_rows.shape
    blocks = sections * cp_count
    tokens = own_rows * blocks

    y_count = cp_count // 4
    me_section = lax.axis_index("section")
    me_cp = lax.axis_index("cp")
    me_core = me_cp % 2
    me_y = me_cp // 4
    me_z = me_cp // 2 % 2
    me_ring = me_z * 2 + me_section
    flat = sections * cp_count
    axes = ("section", "cp")

    def coords(g):
        c = g % cp_count
        return g // cp_count, c // 4, c // 2 % 2, c % 2

    def linear(s_i, y_i, z_i, core_i):
        return s_i * cp_count + y_i * 4 + z_i * 2 + core_i

    def ring_perm(step):
        pairs = []
        for g in range(flat):
            s_i, y_i, z_i, core_i = coords(g)
            ring = (z_i * 2 + s_i + step) % 4
            pairs.append((g, linear(ring % 2, y_i, ring // 2, core_i)))
        return pairs

    def y_perm(step):
        pairs = []
        for g in range(flat):
            s_i, y_i, z_i, core_i = coords(g)
            pairs.append((g, linear(s_i, (y_i + step) % y_count, z_i, core_i)))
        return pairs

    pair_perm = [(g, g ^ 1) for g in range(flat)]

    def gather_rows(local):
        ring_parts = [local] + [lax.ppermute(local, axes, ring_perm(k)) for k in range(1, 4)]
        ring_stack = jnp.stack(ring_parts)
        y_parts = [ring_stack] + [
            lax.ppermute(ring_stack, axes, y_perm(k)) for k in range(1, y_count)
        ]
        y_stack = jnp.stack(y_parts)
        both = jnp.stack([y_stack, lax.ppermute(y_stack, axes, pair_perm)])
        return both.reshape(-1, local.shape[-1])

    kc = jnp.arange(2, dtype=jnp.int32)[:, None, None]
    ky = jnp.arange(y_count, dtype=jnp.int32)[None, :, None]
    kz = jnp.arange(4, dtype=jnp.int32)[None, None, :]
    src_ring = (me_ring - kz) % 4
    actor_of = (
        (src_ring % 2) * cp_count
        + ((me_y - ky) % y_count) * 4
        + (src_ring // 2) * 2
        + (me_core ^ kc)
    ).reshape(blocks)
    front_chunks = 1
    half = own_rows // front_chunks
    rows_parts = [
        gather_rows(rollout_rows[part * half : (part + 1) * half]) for part in range(front_chunks)
    ]

    block_ids = jnp.arange(blocks, dtype=jnp.int32)
    packed_block = jnp.sum(
        jnp.where(block_owner[None, :] == block_ids[:, None], block_ids[None, :], 0), axis=1
    )
    inner = jnp.arange(own_rows, dtype=jnp.int32)
    half_inner = jnp.arange(half, dtype=jnp.int32)
    layout_start = packed_block[actor_of] * own_rows
    position = jnp.concatenate(
        [
            (layout_start[:, None] + part * half + half_inner[None, :]).reshape(-1)
            for part in range(front_chunks)
        ]
    )
    query_order = (
        packed_block.reshape(sections, y_count, 2, 2).transpose(3, 1, 2, 0).reshape(blocks)
    )
    query_position = (query_order[:, None] * own_rows + inner[None, :]).reshape(tokens)
    seq_ends = jnp.cumsum(lengths)
    sequence = jnp.sum((position[:, None] >= seq_ends[None, :]).astype(jnp.int32), axis=1)
    query_sequence = jnp.sum(
        (query_position[:, None] >= seq_ends[None, :]).astype(jnp.int32), axis=1
    )

    me_tp = lax.axis_index("tp")
    qkv_weights = w_qkv[0]

    def project(rows_in):
        rows_f32 = rows_in.astype(jnp.float32)
        squares = jnp.sum(jnp.square(rows_f32), axis=1)
        total_squares = squares
        for step in range(1, tp_count):
            total_squares = total_squares + shifted(squares, "tp", tp_count, step)
        inverse_rms = lax.rsqrt(total_squares / D + 1e-05)
        scaled = (rows_f32 * norm_gain[0][None, :]).astype(jnp.bfloat16)

        def head_partial(head):
            head_weights = lax.dynamic_slice_in_dim(qkv_weights, head * HEAD, HEAD, axis=2)
            return jnp.einsum(
                "rd,kde->kre", scaled, head_weights, preferred_element_type=jnp.float32
            )

        summed = head_partial(me_tp)
        for step in range(1, tp_count):
            piece = head_partial((me_tp + step) % tp_count).astype(jnp.bfloat16)
            summed = summed + shifted(piece, "tp", tp_count, step).astype(jnp.float32)
        return (summed * inverse_rms[None, :, None]).astype(jnp.bfloat16)

    qkv_parts = [project(part) for part in rows_parts]
    key_rows = jnp.concatenate([part[1] for part in qkv_parts], axis=0)
    value_rows = jnp.concatenate([part[2] for part in qkv_parts], axis=0)
    t_core = jnp.arange(2, dtype=jnp.int32)[:, None, None, None]
    t_y = jnp.arange(y_count, dtype=jnp.int32)[None, :, None, None]
    t_z = jnp.arange(2, dtype=jnp.int32)[None, None, :, None]
    t_s = jnp.arange(sections, dtype=jnp.int32)[None, None, None, :]
    layout_of = (
        ((t_core ^ me_core) * y_count + (me_y - t_y) % y_count) * 4
        + (me_ring - (t_z * 2 + t_s)) % 4
    ).reshape(blocks)
    queries = jnp.concatenate(
        [jnp.take(part[0].reshape(blocks, half, HEAD), layout_of, axis=0) for part in qkv_parts],
        axis=1,
    ).reshape(tokens, HEAD)

    out_weight = w_out[0].reshape(tp_count, HEAD, width_here)
    source_of = (me_tp - jnp.arange(tp_count, dtype=jnp.int32)) % tp_count
    out_weight = jnp.take(out_weight, source_of, axis=0)
    z_flip = [(g, g // cp_count * cp_count + (g % cp_count ^ 2)) for g in range(flat)]
    s_flip = [(g, (g + cp_count) % flat) for g in range(flat)]
    both_flip = [
        (g, (g + cp_count) % flat // cp_count * cp_count + (g % cp_count ^ 2)) for g in range(flat)
    ]
    core_perm = [(c, c ^ 1) for c in range(cp_count)]

    def back_half(chunk_queries, chunk_position, chunk_sequence):
        chunk_rows = chunk_queries.shape[0] // blocks
        allowed = (chunk_sequence[:, None] == sequence[None, :]) & (
            position[None, :] <= chunk_position[:, None]
        )
        scores = jnp.dot(chunk_queries, key_rows.T, preferred_element_type=jnp.float32)
        scores = jnp.where(allowed, scores / math.sqrt(HEAD), -1e30)
        row_peak = jnp.max(scores, axis=1, keepdims=True)
        weights = jnp.where(allowed, jnp.exp(scores - row_peak), 0.0)
        row_total = jnp.sum(weights, axis=1, keepdims=True)
        probabilities = weights.astype(jnp.bfloat16)
        mixed = jnp.dot(probabilities, value_rows, preferred_element_type=jnp.float32)
        attended = (mixed / row_total).astype(jnp.bfloat16)
        parts = [attended] + [
            shifted(attended, "tp", tp_count, step) for step in range(1, tp_count)
        ]
        partial_out = jnp.einsum(
            "kre,kew->rw", jnp.stack(parts), out_weight, preferred_element_type=jnp.float32
        ).astype(jnp.bfloat16)
        staged = partial_out.reshape(2, y_count, 2, sections, chunk_rows, width_here)
        kept = lax.dynamic_index_in_dim(staged, me_core, 0, keepdims=False)
        given = lax.dynamic_index_in_dim(staged, 1 - me_core, 0, keepdims=False)
        chip_sum = kept.astype(jnp.float32) + lax.ppermute(given, "cp", core_perm).astype(
            jnp.float32
        )
        chip_half = chip_sum.astype(jnp.bfloat16)
        y_sum = lax.dynamic_index_in_dim(chip_sum, me_y, 0, keepdims=False)
        for step in range(1, y_count):
            piece = lax.dynamic_index_in_dim(
                chip_half, (me_y + step) % y_count, 0, keepdims=False
            )
            y_perm = [(c, ((c // 4 + step) % y_count) * 4 + c % 4) for c in range(cp_count)]
            y_sum = y_sum + lax.ppermute(piece, "cp", y_perm).astype(jnp.float32)
        y_half = y_sum.astype(jnp.bfloat16)

        def piece_of(z_index, section_index):
            z_part = lax.dynamic_index_in_dim(y_half, z_index, 0, keepdims=False)
            return lax.dynamic_index_in_dim(z_part, section_index, 0, keepdims=False)

        own_part = lax.dynamic_index_in_dim(
            lax.dynamic_index_in_dim(y_sum, me_z, 0, keepdims=False), me_section, 0, keepdims=False
        )
        own_total = own_part + lax.ppermute(piece_of(1 - me_z, me_section), axes, z_flip).astype(
            jnp.float32
        )
        other_total = lax.ppermute(piece_of(me_z, 1 - me_section), axes, s_flip).astype(
            jnp.float32
        ) + lax.ppermute(piece_of(1 - me_z, 1 - me_section), axes, both_flip).astype(jnp.float32)
        return own_total.astype(jnp.bfloat16), other_total.astype(jnp.bfloat16)

    chunks = 2
    chunk_rows = own_rows // chunks
    query_blocks = queries.reshape(blocks, own_rows, HEAD)
    position_blocks = query_position.reshape(blocks, own_rows)
    sequence_blocks = query_sequence.reshape(blocks, own_rows)
    own_parts, other_parts = [], []
    for chunk in range(chunks):
        rows_of = slice(chunk * chunk_rows, (chunk + 1) * chunk_rows)
        own_part, other_part = back_half(
            query_blocks[:, rows_of].reshape(-1, HEAD),
            position_blocks[:, rows_of].reshape(-1),
            sequence_blocks[:, rows_of].reshape(-1),
        )
        own_parts.append(own_part)
        other_parts.append(other_part)
    own_total = jnp.concatenate(own_parts, axis=0)
    other_total = jnp.concatenate(other_parts, axis=0)
    return jnp.where(
        me_section == 0, jnp.stack([own_total, other_total]), jnp.stack([other_total, own_total])
    )

def solution(mesh):
    return jax.shard_map(
        on_device,
        mesh=mesh,
        in_specs=(
            P(("section", "cp"), "tp"),
            P(),
            P(),
            P("section", "tp"),
            P("section", None, "tp", "cp"),
            P("section", "cp", "tp"),
        ),
        out_specs=P(None, ("section", "cp"), "tp"),
        check_vma=False,
    )
```

```python
import math

import jax
import jax.numpy as jnp
from jax import lax
from jax.sharding import PartitionSpec as P

D = 8192
HEAD = 128


def shifted(value, axis, count, step):
    return lax.ppermute(value, axis, perm=[(j, (j + step) % count) for j in range(count)])


def on_device(rollout_rows, lengths, block_owner, norm_gain, w_qkv, w_out):
    tp_count = lax.axis_size("tp")
    cp_count = lax.axis_size("cp")
    sections = lax.axis_size("section")
    own_rows, width_here = rollout_rows.shape
    blocks = sections * cp_count
    tokens = own_rows * blocks

    y_count = cp_count // 4
    me_section = lax.axis_index("section")
    me_cp = lax.axis_index("cp")
    me_core = me_cp % 2
    me_y = me_cp // 4
    me_z = me_cp // 2 % 2
    me_ring = me_z * 2 + me_section
    flat = sections * cp_count
    axes = ("section", "cp")

    def coords(g):
        c = g % cp_count
        return g // cp_count, c // 4, c // 2 % 2, c % 2

    def linear(s_i, y_i, z_i, core_i):
        return s_i * cp_count + y_i * 4 + z_i * 2 + core_i

    def ring_perm(step):
        pairs = []
        for g in range(flat):
            s_i, y_i, z_i, core_i = coords(g)
            ring = (z_i * 2 + s_i + step) % 4
            pairs.append((g, linear(ring % 2, y_i, ring // 2, core_i)))
        return pairs

    def y_perm(step):
        pairs = []
        for g in range(flat):
            s_i, y_i, z_i, core_i = coords(g)
            pairs.append((g, linear(s_i, (y_i + step) % y_count, z_i, core_i)))
        return pairs

    pair_perm = [(g, g ^ 1) for g in range(flat)]

    def gather_rows(local):
        ring_parts = [local] + [lax.ppermute(local, axes, ring_perm(k)) for k in range(1, 4)]
        ring_stack = jnp.stack(ring_parts)
        y_parts = [ring_stack] + [
            lax.ppermute(ring_stack, axes, y_perm(k)) for k in range(1, y_count)
        ]
        y_stack = jnp.stack(y_parts)
        both = jnp.stack([y_stack, lax.ppermute(y_stack, axes, pair_perm)])
        return both.reshape(-1, local.shape[-1])

    kc = jnp.arange(2, dtype=jnp.int32)[:, None, None]
    ky = jnp.arange(y_count, dtype=jnp.int32)[None, :, None]
    kz = jnp.arange(4, dtype=jnp.int32)[None, None, :]
    src_ring = (me_ring - kz) % 4
    actor_of = (
        (src_ring % 2) * cp_count
        + ((me_y - ky) % y_count) * 4
        + (src_ring // 2) * 2
        + (me_core ^ kc)
    ).reshape(blocks)
    half = own_rows // 2
    rows_parts = [gather_rows(rollout_rows[:half]), gather_rows(rollout_rows[half:])]

    block_ids = jnp.arange(blocks, dtype=jnp.int32)
    packed_block = jnp.sum(
        jnp.where(block_owner[None, :] == block_ids[:, None], block_ids[None, :], 0), axis=1
    )
    inner = jnp.arange(own_rows, dtype=jnp.int32)
    half_inner = jnp.arange(half, dtype=jnp.int32)
    layout_start = packed_block[actor_of] * own_rows
    position = jnp.concatenate(
        [
            (layout_start[:, None] + half_inner[None, :]).reshape(-1),
            (layout_start[:, None] + half + half_inner[None, :]).reshape(-1),
        ]
    )
    query_order = (
        packed_block.reshape(sections, y_count, 2, 2).transpose(3, 1, 2, 0).reshape(blocks)
    )
    query_position = (query_order[:, None] * own_rows + inner[None, :]).reshape(tokens)
    seq_ends = jnp.cumsum(lengths)
    sequence = jnp.sum((position[:, None] >= seq_ends[None, :]).astype(jnp.int32), axis=1)
    query_sequence = jnp.sum(
        (query_position[:, None] >= seq_ends[None, :]).astype(jnp.int32), axis=1
    )

    me_tp = lax.axis_index("tp")
    qkv_weights = w_qkv[0]

    def project(rows_in):
        rows_f32 = rows_in.astype(jnp.float32)
        squares = jnp.sum(jnp.square(rows_f32), axis=1)
        total_squares = squares
        for step in range(1, tp_count):
            total_squares = total_squares + shifted(squares, "tp", tp_count, step)
        inverse_rms = lax.rsqrt(total_squares / D + 1e-05)
        scaled = (rows_f32 * norm_gain[0][None, :]).astype(jnp.bfloat16)

        def head_partial(head):
            head_weights = lax.dynamic_slice_in_dim(qkv_weights, head * HEAD, HEAD, axis=2)
            return jnp.einsum(
                "rd,kde->kre", scaled, head_weights, preferred_element_type=jnp.float32
            )

        summed = lax.optimization_barrier(head_partial(me_tp))
        for step in range(1, tp_count):
            piece = head_partial((me_tp + step) % tp_count).astype(jnp.bfloat16)
            summed = summed + shifted(piece, "tp", tp_count, step).astype(jnp.float32)
        return (summed * inverse_rms[None, :, None]).astype(jnp.bfloat16)

    qkv_parts = [project(part) for part in rows_parts]
    key_rows = jnp.concatenate([part[1] for part in qkv_parts], axis=0)
    value_rows = jnp.concatenate([part[2] for part in qkv_parts], axis=0)
    t_core = jnp.arange(2, dtype=jnp.int32)[:, None, None, None]
    t_y = jnp.arange(y_count, dtype=jnp.int32)[None, :, None, None]
    t_z = jnp.arange(2, dtype=jnp.int32)[None, None, :, None]
    t_s = jnp.arange(sections, dtype=jnp.int32)[None, None, None, :]
    layout_of = (
        ((t_core ^ me_core) * y_count + (me_y - t_y) % y_count) * 4
        + (me_ring - (t_z * 2 + t_s)) % 4
    ).reshape(blocks)
    queries = jnp.concatenate(
        [jnp.take(part[0].reshape(blocks, half, HEAD), layout_of, axis=0) for part in qkv_parts],
        axis=1,
    ).reshape(tokens, HEAD)

    out_weight = w_out[0].reshape(tp_count, HEAD, width_here)
    source_of = (me_tp - jnp.arange(tp_count, dtype=jnp.int32)) % tp_count
    out_weight = jnp.take(out_weight, source_of, axis=0)
    z_flip = [(g, g // cp_count * cp_count + (g % cp_count ^ 2)) for g in range(flat)]
    s_flip = [(g, (g + cp_count) % flat) for g in range(flat)]
    both_flip = [
        (g, (g + cp_count) % flat // cp_count * cp_count + (g % cp_count ^ 2)) for g in range(flat)
    ]
    core_perm = [(c, c ^ 1) for c in range(cp_count)]

    def back_half(chunk_queries, chunk_position, chunk_sequence):
        chunk_rows = chunk_queries.shape[0] // blocks
        allowed = (chunk_sequence[:, None] == sequence[None, :]) & (
            position[None, :] <= chunk_position[:, None]
        )
        scores = jnp.dot(chunk_queries, key_rows.T, preferred_element_type=jnp.float32)
        scores = jnp.where(allowed, scores / math.sqrt(HEAD), -1e30)
        row_peak = jnp.max(scores, axis=1, keepdims=True)
        weights = jnp.where(allowed, jnp.exp(scores - row_peak), 0.0)
        row_total = jnp.sum(weights, axis=1, keepdims=True)
        probabilities = weights.astype(jnp.bfloat16)
        mixed = jnp.dot(probabilities, value_rows, preferred_element_type=jnp.float32)
        attended = (mixed / row_total).astype(jnp.bfloat16)
        parts = [attended] + [
            shifted(attended, "tp", tp_count, step) for step in range(1, tp_count)
        ]
        partial_out = jnp.einsum(
            "kre,kew->rw", jnp.stack(parts), out_weight, preferred_element_type=jnp.float32
        ).astype(jnp.bfloat16)
        staged = partial_out.reshape(2, y_count, 2, sections, chunk_rows, width_here)
        kept = lax.dynamic_index_in_dim(staged, me_core, 0, keepdims=False)
        given = lax.dynamic_index_in_dim(staged, 1 - me_core, 0, keepdims=False)
        chip_sum = kept.astype(jnp.float32) + lax.ppermute(given, "cp", core_perm).astype(
            jnp.float32
        )
        chip_half = chip_sum.astype(jnp.bfloat16)
        y_sum = lax.dynamic_index_in_dim(chip_sum, me_y, 0, keepdims=False)
        for step in range(1, y_count):
            piece = lax.dynamic_index_in_dim(
                chip_half, (me_y + step) % y_count, 0, keepdims=False
            )
            y_perm = [(c, ((c // 4 + step) % y_count) * 4 + c % 4) for c in range(cp_count)]
            y_sum = y_sum + lax.ppermute(piece, "cp", y_perm).astype(jnp.float32)
        y_half = y_sum.astype(jnp.bfloat16)

        def piece_of(z_index, section_index):
            z_part = lax.dynamic_index_in_dim(y_half, z_index, 0, keepdims=False)
            return lax.dynamic_index_in_dim(z_part, section_index, 0, keepdims=False)

        own_part = lax.dynamic_index_in_dim(
            lax.dynamic_index_in_dim(y_sum, me_z, 0, keepdims=False), me_section, 0, keepdims=False
        )
        own_total = own_part + lax.ppermute(piece_of(1 - me_z, me_section), axes, z_flip).astype(
            jnp.float32
        )
        other_total = lax.ppermute(piece_of(me_z, 1 - me_section), axes, s_flip).astype(
            jnp.float32
        ) + lax.ppermute(piece_of(1 - me_z, 1 - me_section), axes, both_flip).astype(jnp.float32)
        return own_total.astype(jnp.bfloat16), other_total.astype(jnp.bfloat16)

    chunks = 2
    chunk_rows = own_rows // chunks
    query_blocks = queries.reshape(blocks, own_rows, HEAD)
    position_blocks = query_position.reshape(blocks, own_rows)
    sequence_blocks = query_sequence.reshape(blocks, own_rows)
    own_parts, other_parts = [], []
    for chunk in range(chunks):
        rows_of = slice(chunk * chunk_rows, (chunk + 1) * chunk_rows)
        own_part, other_part = back_half(
            query_blocks[:, rows_of].reshape(-1, HEAD),
            position_blocks[:, rows_of].reshape(-1),
            sequence_blocks[:, rows_of].reshape(-1),
        )
        own_parts.append(own_part)
        other_parts.append(other_part)
    own_total = jnp.concatenate(own_parts, axis=0)
    other_total = jnp.concatenate(other_parts, axis=0)
    return jnp.where(
        me_section == 0, jnp.stack([own_total, other_total]), jnp.stack([other_total, own_total])
    )

def solution(mesh):
    return jax.shard_map(
        on_device,
        mesh=mesh,
        in_specs=(
            P(("section", "cp"), "tp"),
            P(),
            P(),
            P("section", "tp"),
            P("section", None, "tp", "cp"),
            P("section", "cp", "tp"),
        ),
        out_specs=P(None, ("section", "cp"), "tp"),
        check_vma=False,
    )
```

```python
import math

import jax
import jax.numpy as jnp
from jax import lax
from jax.sharding import PartitionSpec as P

D = 8192
HEAD = 128


def shifted(value, axis, count, step):
    return lax.ppermute(value, axis, perm=[(j, (j + step) % count) for j in range(count)])


def on_device(rollout_rows, lengths, block_owner, norm_gain, w_qkv, w_out):
    tp_count = lax.axis_size("tp")
    cp_count = lax.axis_size("cp")
    sections = lax.axis_size("section")
    own_rows, width_here = rollout_rows.shape
    blocks = sections * cp_count
    tokens = own_rows * blocks

    y_count = cp_count // 4
    me_section = lax.axis_index("section")
    me_cp = lax.axis_index("cp")
    me_core = me_cp % 2
    me_y = me_cp // 4
    me_z = me_cp // 2 % 2
    me_ring = me_z * 2 + me_section
    flat = sections * cp_count
    axes = ("section", "cp")

    def coords(g):
        c = g % cp_count
        return g // cp_count, c // 4, c // 2 % 2, c % 2

    def linear(s_i, y_i, z_i, core_i):
        return s_i * cp_count + y_i * 4 + z_i * 2 + core_i

    def ring_perm(step):
        pairs = []
        for g in range(flat):
            s_i, y_i, z_i, core_i = coords(g)
            ring = (z_i * 2 + s_i + step) % 4
            pairs.append((g, linear(ring % 2, y_i, ring // 2, core_i)))
        return pairs

    def y_perm(step):
        pairs = []
        for g in range(flat):
            s_i, y_i, z_i, core_i = coords(g)
            pairs.append((g, linear(s_i, (y_i + step) % y_count, z_i, core_i)))
        return pairs

    pair_perm = [(g, g ^ 1) for g in range(flat)]

    def gather_rows(local):
        split = local.shape[-1] // 2
        first, second = local[:, :split], local[:, split:]
        ring_parts = [first] + [lax.ppermute(first, axes, ring_perm(k)) for k in range(1, 4)]
        ring_stack = jnp.stack(ring_parts)
        z_then_y = jnp.stack(
            [ring_stack]
            + [lax.ppermute(ring_stack, axes, y_perm(k)) for k in range(1, y_count)]
        )
        y_parts = [second] + [lax.ppermute(second, axes, y_perm(k)) for k in range(1, y_count)]
        y_stack = jnp.stack(y_parts)
        y_then_z = jnp.stack(
            [y_stack] + [lax.ppermute(y_stack, axes, ring_perm(k)) for k in range(1, 4)]
        ).swapaxes(0, 1)
        gathered = jnp.concatenate([z_then_y, y_then_z], axis=-1)
        both = jnp.stack([gathered, lax.ppermute(gathered, axes, pair_perm)])
        return both.reshape(-1, local.shape[-1])

    kc = jnp.arange(2, dtype=jnp.int32)[:, None, None]
    ky = jnp.arange(y_count, dtype=jnp.int32)[None, :, None]
    kz = jnp.arange(4, dtype=jnp.int32)[None, None, :]
    src_ring = (me_ring - kz) % 4
    actor_of = (
        (src_ring % 2) * cp_count
        + ((me_y - ky) % y_count) * 4
        + (src_ring // 2) * 2
        + (me_core ^ kc)
    ).reshape(blocks)
    half = own_rows // 2
    rows_parts = [gather_rows(rollout_rows[:half]), gather_rows(rollout_rows[half:])]

    block_ids = jnp.arange(blocks, dtype=jnp.int32)
    packed_block = jnp.sum(
        jnp.where(block_owner[None, :] == block_ids[:, None], block_ids[None, :], 0), axis=1
    )
    inner = jnp.arange(own_rows, dtype=jnp.int32)
    half_inner = jnp.arange(half, dtype=jnp.int32)
    layout_start = packed_block[actor_of] * own_rows
    position = jnp.concatenate(
        [
            (layout_start[:, None] + half_inner[None, :]).reshape(-1),
            (layout_start[:, None] + half + half_inner[None, :]).reshape(-1),
        ]
    )
    query_order = (
        packed_block.reshape(sections, y_count, 2, 2).transpose(3, 1, 2, 0).reshape(blocks)
    )
    query_position = (query_order[:, None] * own_rows + inner[None, :]).reshape(tokens)
    seq_ends = jnp.cumsum(lengths)
    sequence = jnp.sum((position[:, None] >= seq_ends[None, :]).astype(jnp.int32), axis=1)
    query_sequence = jnp.sum(
        (query_position[:, None] >= seq_ends[None, :]).astype(jnp.int32), axis=1
    )

    me_tp = lax.axis_index("tp")
    qkv_weights = w_qkv[0]

    def project(rows_in):
        rows_f32 = rows_in.astype(jnp.float32)
        squares = jnp.sum(jnp.square(rows_f32), axis=1)
        total_squares = squares
        for step in range(1, tp_count):
            total_squares = total_squares + shifted(squares, "tp", tp_count, step)
        inverse_rms = lax.rsqrt(total_squares / D + 1e-05)
        scaled = (rows_f32 * norm_gain[0][None, :]).astype(jnp.bfloat16)

        def head_partial(head):
            head_weights = lax.dynamic_slice_in_dim(qkv_weights, head * HEAD, HEAD, axis=2)
            return jnp.einsum(
                "rd,kde->kre", scaled, head_weights, preferred_element_type=jnp.float32
            )

        summed = head_partial(me_tp)
        for step in range(1, tp_count):
            piece = head_partial((me_tp + step) % tp_count).astype(jnp.bfloat16)
            summed = summed + shifted(piece, "tp", tp_count, step).astype(jnp.float32)
        return (summed * inverse_rms[None, :, None]).astype(jnp.bfloat16)

    qkv_parts = [project(part) for part in rows_parts]
    key_rows = jnp.concatenate([part[1] for part in qkv_parts], axis=0)
    value_rows = jnp.concatenate([part[2] for part in qkv_parts], axis=0)
    t_core = jnp.arange(2, dtype=jnp.int32)[:, None, None, None]
    t_y = jnp.arange(y_count, dtype=jnp.int32)[None, :, None, None]
    t_z = jnp.arange(2, dtype=jnp.int32)[None, None, :, None]
    t_s = jnp.arange(sections, dtype=jnp.int32)[None, None, None, :]
    layout_of = (
        ((t_core ^ me_core) * y_count + (me_y - t_y) % y_count) * 4
        + (me_ring - (t_z * 2 + t_s)) % 4
    ).reshape(blocks)
    queries = jnp.concatenate(
        [jnp.take(part[0].reshape(blocks, half, HEAD), layout_of, axis=0) for part in qkv_parts],
        axis=1,
    ).reshape(tokens, HEAD)

    out_weight = w_out[0].reshape(tp_count, HEAD, width_here)
    source_of = (me_tp - jnp.arange(tp_count, dtype=jnp.int32)) % tp_count
    out_weight = jnp.take(out_weight, source_of, axis=0)
    z_flip = [(g, g // cp_count * cp_count + (g % cp_count ^ 2)) for g in range(flat)]
    s_flip = [(g, (g + cp_count) % flat) for g in range(flat)]
    both_flip = [
        (g, (g + cp_count) % flat // cp_count * cp_count + (g % cp_count ^ 2)) for g in range(flat)
    ]
    core_perm = [(c, c ^ 1) for c in range(cp_count)]

    def back_half(chunk_queries, chunk_position, chunk_sequence):
        chunk_rows = chunk_queries.shape[0] // blocks
        allowed = (chunk_sequence[:, None] == sequence[None, :]) & (
            position[None, :] <= chunk_position[:, None]
        )
        scores = jnp.dot(chunk_queries, key_rows.T, preferred_element_type=jnp.float32)
        scores = jnp.where(allowed, scores / math.sqrt(HEAD), -1e30)
        row_peak = jnp.max(scores, axis=1, keepdims=True)
        weights = jnp.where(allowed, jnp.exp(scores - row_peak), 0.0)
        row_total = jnp.sum(weights, axis=1, keepdims=True)
        probabilities = weights.astype(jnp.bfloat16)
        mixed = jnp.dot(probabilities, value_rows, preferred_element_type=jnp.float32)
        attended = (mixed / row_total).astype(jnp.bfloat16)
        parts = [attended] + [
            shifted(attended, "tp", tp_count, step) for step in range(1, tp_count)
        ]
        partial_out = jnp.einsum(
            "kre,kew->rw", jnp.stack(parts), out_weight, preferred_element_type=jnp.float32
        ).astype(jnp.bfloat16)
        staged = partial_out.reshape(2, y_count, 2, sections, chunk_rows, width_here)
        kept = lax.dynamic_index_in_dim(staged, me_core, 0, keepdims=False)
        given = lax.dynamic_index_in_dim(staged, 1 - me_core, 0, keepdims=False)
        chip_sum = kept.astype(jnp.float32) + lax.ppermute(given, "cp", core_perm).astype(
            jnp.float32
        )
        chip_half = chip_sum.astype(jnp.bfloat16)
        y_sum = lax.dynamic_index_in_dim(chip_sum, me_y, 0, keepdims=False)
        for step in range(1, y_count):
            piece = lax.dynamic_index_in_dim(
                chip_half, (me_y + step) % y_count, 0, keepdims=False
            )
            y_perm = [(c, ((c // 4 + step) % y_count) * 4 + c % 4) for c in range(cp_count)]
            y_sum = y_sum + lax.ppermute(piece, "cp", y_perm).astype(jnp.float32)
        y_half = y_sum.astype(jnp.bfloat16)

        def piece_of(z_index, section_index):
            z_part = lax.dynamic_index_in_dim(y_half, z_index, 0, keepdims=False)
            return lax.dynamic_index_in_dim(z_part, section_index, 0, keepdims=False)

        own_part = lax.dynamic_index_in_dim(
            lax.dynamic_index_in_dim(y_sum, me_z, 0, keepdims=False), me_section, 0, keepdims=False
        )
        own_total = own_part + lax.ppermute(piece_of(1 - me_z, me_section), axes, z_flip).astype(
            jnp.float32
        )
        other_total = lax.ppermute(piece_of(me_z, 1 - me_section), axes, s_flip).astype(
            jnp.float32
        ) + lax.ppermute(piece_of(1 - me_z, 1 - me_section), axes, both_flip).astype(jnp.float32)
        return own_total.astype(jnp.bfloat16), other_total.astype(jnp.bfloat16)

    chunks = 2
    chunk_rows = own_rows // chunks
    query_blocks = queries.reshape(blocks, own_rows, HEAD)
    position_blocks = query_position.reshape(blocks, own_rows)
    sequence_blocks = query_sequence.reshape(blocks, own_rows)
    own_parts, other_parts = [], []
    for chunk in range(chunks):
        rows_of = slice(chunk * chunk_rows, (chunk + 1) * chunk_rows)
        own_part, other_part = back_half(
            query_blocks[:, rows_of].reshape(-1, HEAD),
            position_blocks[:, rows_of].reshape(-1),
            sequence_blocks[:, rows_of].reshape(-1),
        )
        own_parts.append(own_part)
        other_parts.append(other_part)
    own_total = jnp.concatenate(own_parts, axis=0)
    other_total = jnp.concatenate(other_parts, axis=0)
    return jnp.where(
        me_section == 0, jnp.stack([own_total, other_total]), jnp.stack([other_total, own_total])
    )

def solution(mesh):
    return jax.shard_map(
        on_device,
        mesh=mesh,
        in_specs=(
            P(("section", "cp"), "tp"),
            P(),
            P(),
            P("section", "tp"),
            P("section", None, "tp", "cp"),
            P("section", "cp", "tp"),
        ),
        out_specs=P(None, ("section", "cp"), "tp"),
        check_vma=False,
    )
```

```python
import math

import jax
import jax.numpy as jnp
from jax import lax
from jax.sharding import PartitionSpec as P

D = 8192
HEAD = 128


def shifted(value, axis, count, step):
    return lax.ppermute(value, axis, perm=[(j, (j + step) % count) for j in range(count)])


def on_device(rollout_rows, lengths, block_owner, norm_gain, w_qkv, w_out):
    tp_count = lax.axis_size("tp")
    cp_count = lax.axis_size("cp")
    sections = lax.axis_size("section")
    own_rows, width_here = rollout_rows.shape
    blocks = sections * cp_count
    tokens = own_rows * blocks

    y_count = cp_count // 4
    me_section = lax.axis_index("section")
    me_cp = lax.axis_index("cp")
    me_core = me_cp % 2
    me_y = me_cp // 4
    me_z = me_cp // 2 % 2
    me_ring = me_z * 2 + me_section
    flat = sections * cp_count
    axes = ("section", "cp")

    def coords(g):
        c = g % cp_count
        return g // cp_count, c // 4, c // 2 % 2, c % 2

    def linear(s_i, y_i, z_i, core_i):
        return s_i * cp_count + y_i * 4 + z_i * 2 + core_i

    def ring_perm(step):
        pairs = []
        for g in range(flat):
            s_i, y_i, z_i, core_i = coords(g)
            ring = (z_i * 2 + s_i + step) % 4
            pairs.append((g, linear(ring % 2, y_i, ring // 2, core_i)))
        return pairs

    def y_perm(step):
        pairs = []
        for g in range(flat):
            s_i, y_i, z_i, core_i = coords(g)
            pairs.append((g, linear(s_i, (y_i + step) % y_count, z_i, core_i)))
        return pairs

    pair_perm = [(g, g ^ 1) for g in range(flat)]

    def two_y_hops(value, perm_axes, forward, backward):
        split = value.shape[-1] // 2
        ahead = lax.ppermute(lax.ppermute(value[..., :split], perm_axes, forward), perm_axes, forward)
        behind = lax.ppermute(
            lax.ppermute(value[..., split:], perm_axes, backward), perm_axes, backward
        )
        return jnp.concatenate([ahead, behind], axis=-1)

    def y_shift(value, step):
        if step == 2 and y_count == 4:
            return two_y_hops(value, axes, y_perm(1), y_perm(3))
        return lax.ppermute(value, axes, y_perm(step))

    def gather_rows(local):
        ring_parts = [local] + [lax.ppermute(local, axes, ring_perm(k)) for k in range(1, 4)]
        ring_stack = jnp.stack(ring_parts)
        y_parts = [ring_stack] + [y_shift(ring_stack, k) for k in range(1, y_count)]
        y_stack = jnp.stack(y_parts)
        both = jnp.stack([y_stack, lax.ppermute(y_stack, axes, pair_perm)])
        return both.reshape(-1, local.shape[-1])

    kc = jnp.arange(2, dtype=jnp.int32)[:, None, None]
    ky = jnp.arange(y_count, dtype=jnp.int32)[None, :, None]
    kz = jnp.arange(4, dtype=jnp.int32)[None, None, :]
    src_ring = (me_ring - kz) % 4
    actor_of = (
        (src_ring % 2) * cp_count
        + ((me_y - ky) % y_count) * 4
        + (src_ring // 2) * 2
        + (me_core ^ kc)
    ).reshape(blocks)
    half = own_rows // 2
    rows_parts = [gather_rows(rollout_rows[:half]), gather_rows(rollout_rows[half:])]

    block_ids = jnp.arange(blocks, dtype=jnp.int32)
    packed_block = jnp.sum(
        jnp.where(block_owner[None, :] == block_ids[:, None], block_ids[None, :], 0), axis=1
    )
    inner = jnp.arange(own_rows, dtype=jnp.int32)
    half_inner = jnp.arange(half, dtype=jnp.int32)
    layout_start = packed_block[actor_of] * own_rows
    position = jnp.concatenate(
        [
            (layout_start[:, None] + half_inner[None, :]).reshape(-1),
            (layout_start[:, None] + half + half_inner[None, :]).reshape(-1),
        ]
    )
    query_order = (
        packed_block.reshape(sections, y_count, 2, 2).transpose(3, 1, 2, 0).reshape(blocks)
    )
    query_position = (query_order[:, None] * own_rows + inner[None, :]).reshape(tokens)
    seq_ends = jnp.cumsum(lengths)
    sequence = jnp.sum((position[:, None] >= seq_ends[None, :]).astype(jnp.int32), axis=1)
    query_sequence = jnp.sum(
        (query_position[:, None] >= seq_ends[None, :]).astype(jnp.int32), axis=1
    )

    me_tp = lax.axis_index("tp")
    qkv_weights = w_qkv[0]

    def project(rows_in):
        rows_f32 = rows_in.astype(jnp.float32)
        squares = jnp.sum(jnp.square(rows_f32), axis=1)
        total_squares = squares
        for step in range(1, tp_count):
            total_squares = total_squares + shifted(squares, "tp", tp_count, step)
        inverse_rms = lax.rsqrt(total_squares / D + 1e-05)
        scaled = (rows_f32 * norm_gain[0][None, :]).astype(jnp.bfloat16)

        def head_partial(head):
            head_weights = lax.dynamic_slice_in_dim(qkv_weights, head * HEAD, HEAD, axis=2)
            return jnp.einsum(
                "rd,kde->kre", scaled, head_weights, preferred_element_type=jnp.float32
            )

        summed = head_partial(me_tp)
        for step in range(1, tp_count):
            piece = head_partial((me_tp + step) % tp_count).astype(jnp.bfloat16)
            summed = summed + shifted(piece, "tp", tp_count, step).astype(jnp.float32)
        return (summed * inverse_rms[None, :, None]).astype(jnp.bfloat16)

    qkv_parts = [project(part) for part in rows_parts]
    key_rows = jnp.concatenate([part[1] for part in qkv_parts], axis=0)
    value_rows = jnp.concatenate([part[2] for part in qkv_parts], axis=0)
    t_core = jnp.arange(2, dtype=jnp.int32)[:, None, None, None]
    t_y = jnp.arange(y_count, dtype=jnp.int32)[None, :, None, None]
    t_z = jnp.arange(2, dtype=jnp.int32)[None, None, :, None]
    t_s = jnp.arange(sections, dtype=jnp.int32)[None, None, None, :]
    layout_of = (
        ((t_core ^ me_core) * y_count + (me_y - t_y) % y_count) * 4
        + (me_ring - (t_z * 2 + t_s)) % 4
    ).reshape(blocks)
    queries = jnp.concatenate(
        [jnp.take(part[0].reshape(blocks, half, HEAD), layout_of, axis=0) for part in qkv_parts],
        axis=1,
    ).reshape(tokens, HEAD)

    out_weight = w_out[0].reshape(tp_count, HEAD, width_here)
    source_of = (me_tp - jnp.arange(tp_count, dtype=jnp.int32)) % tp_count
    out_weight = jnp.take(out_weight, source_of, axis=0)
    z_flip = [(g, g // cp_count * cp_count + (g % cp_count ^ 2)) for g in range(flat)]
    s_flip = [(g, (g + cp_count) % flat) for g in range(flat)]
    both_flip = [
        (g, (g + cp_count) % flat // cp_count * cp_count + (g % cp_count ^ 2)) for g in range(flat)
    ]
    core_perm = [(c, c ^ 1) for c in range(cp_count)]

    def cp_y_perm(step):
        return [(c, ((c // 4 + step) % y_count) * 4 + c % 4) for c in range(cp_count)]

    def back_half(chunk_queries, chunk_position, chunk_sequence):
        chunk_rows = chunk_queries.shape[0] // blocks
        allowed = (chunk_sequence[:, None] == sequence[None, :]) & (
            position[None, :] <= chunk_position[:, None]
        )
        scores = jnp.dot(chunk_queries, key_rows.T, preferred_element_type=jnp.float32)
        scores = jnp.where(allowed, scores / math.sqrt(HEAD), -1e30)
        row_peak = jnp.max(scores, axis=1, keepdims=True)
        weights = jnp.where(allowed, jnp.exp(scores - row_peak), 0.0)
        row_total = jnp.sum(weights, axis=1, keepdims=True)
        probabilities = weights.astype(jnp.bfloat16)
        mixed = jnp.dot(probabilities, value_rows, preferred_element_type=jnp.float32)
        attended = (mixed / row_total).astype(jnp.bfloat16)
        parts = [attended] + [
            shifted(attended, "tp", tp_count, step) for step in range(1, tp_count)
        ]
        partial_out = jnp.einsum(
            "kre,kew->rw", jnp.stack(parts), out_weight, preferred_element_type=jnp.float32
        ).astype(jnp.bfloat16)
        staged = partial_out.reshape(2, y_count, 2, sections, chunk_rows, width_here)
        kept = lax.dynamic_index_in_dim(staged, me_core, 0, keepdims=False)
        given = lax.dynamic_index_in_dim(staged, 1 - me_core, 0, keepdims=False)
        chip_sum = kept.astype(jnp.float32) + lax.ppermute(given, "cp", core_perm).astype(
            jnp.float32
        )
        chip_half = chip_sum.astype(jnp.bfloat16)
        y_sum = lax.dynamic_index_in_dim(chip_sum, me_y, 0, keepdims=False)
        for step in range(1, y_count):
            piece = lax.dynamic_index_in_dim(
                chip_half, (me_y + step) % y_count, 0, keepdims=False
            )
            if step == 2 and y_count == 4:
                arrived = two_y_hops(piece, "cp", cp_y_perm(1), cp_y_perm(3))
            else:
                arrived = lax.ppermute(piece, "cp", cp_y_perm(step))
            y_sum = y_sum + arrived.astype(jnp.float32)
        y_half = y_sum.astype(jnp.bfloat16)

        def piece_of(z_index, section_index):
            z_part = lax.dynamic_index_in_dim(y_half, z_index, 0, keepdims=False)
            return lax.dynamic_index_in_dim(z_part, section_index, 0, keepdims=False)

        own_part = lax.dynamic_index_in_dim(
            lax.dynamic_index_in_dim(y_sum, me_z, 0, keepdims=False), me_section, 0, keepdims=False
        )
        own_total = own_part + lax.ppermute(piece_of(1 - me_z, me_section), axes, z_flip).astype(
            jnp.float32
        )
        other_total = lax.ppermute(piece_of(me_z, 1 - me_section), axes, s_flip).astype(
            jnp.float32
        ) + lax.ppermute(piece_of(1 - me_z, 1 - me_section), axes, both_flip).astype(jnp.float32)
        return own_total.astype(jnp.bfloat16), other_total.astype(jnp.bfloat16)

    chunks = 2
    chunk_rows = own_rows // chunks
    query_blocks = queries.reshape(blocks, own_rows, HEAD)
    position_blocks = query_position.reshape(blocks, own_rows)
    sequence_blocks = query_sequence.reshape(blocks, own_rows)
    own_parts, other_parts = [], []
    for chunk in range(chunks):
        rows_of = slice(chunk * chunk_rows, (chunk + 1) * chunk_rows)
        own_part, other_part = back_half(
            query_blocks[:, rows_of].reshape(-1, HEAD),
            position_blocks[:, rows_of].reshape(-1),
            sequence_blocks[:, rows_of].reshape(-1),
        )
        own_parts.append(own_part)
        other_parts.append(other_part)
    own_total = jnp.concatenate(own_parts, axis=0)
    other_total = jnp.concatenate(other_parts, axis=0)
    return jnp.where(
        me_section == 0, jnp.stack([own_total, other_total]), jnp.stack([other_total, own_total])
    )

def solution(mesh):
    return jax.shard_map(
        on_device,
        mesh=mesh,
        in_specs=(
            P(("section", "cp"), "tp"),
            P(),
            P(),
            P("section", "tp"),
            P("section", None, "tp", "cp"),
            P("section", "cp", "tp"),
        ),
        out_specs=P(None, ("section", "cp"), "tp"),
        check_vma=False,
    )
```

```python
import math

import jax
import jax.numpy as jnp
from jax import lax
from jax.sharding import PartitionSpec as P

D = 8192
HEAD = 128


def shifted(value, axis, count, step):
    return lax.ppermute(value, axis, perm=[(j, (j + step) % count) for j in range(count)])


def on_device(rollout_rows, lengths, block_owner, norm_gain, w_qkv, w_out):
    tp_count = lax.axis_size("tp")
    cp_count = lax.axis_size("cp")
    sections = lax.axis_size("section")
    own_rows, width_here = rollout_rows.shape
    blocks = sections * cp_count
    tokens = own_rows * blocks

    y_count = cp_count // 4
    me_section = lax.axis_index("section")
    me_cp = lax.axis_index("cp")
    me_core = me_cp % 2
    me_y = me_cp // 4
    me_z = me_cp // 2 % 2
    me_ring = me_z * 2 + me_section
    flat = sections * cp_count
    axes = ("section", "cp")

    def coords(g):
        c = g % cp_count
        return g // cp_count, c // 4, c // 2 % 2, c % 2

    def linear(s_i, y_i, z_i, core_i):
        return s_i * cp_count + y_i * 4 + z_i * 2 + core_i

    def ring_perm(step):
        pairs = []
        for g in range(flat):
            s_i, y_i, z_i, core_i = coords(g)
            ring = (z_i * 2 + s_i + step) % 4
            pairs.append((g, linear(ring % 2, y_i, ring // 2, core_i)))
        return pairs

    def y_perm(step):
        pairs = []
        for g in range(flat):
            s_i, y_i, z_i, core_i = coords(g)
            pairs.append((g, linear(s_i, (y_i + step) % y_count, z_i, core_i)))
        return pairs

    pair_perm = [(g, g ^ 1) for g in range(flat)]

    def gather_rows(local):
        ring_parts = [local] + [lax.ppermute(local, axes, ring_perm(k)) for k in range(1, 4)]
        ring_stack = jnp.stack(ring_parts)
        y_parts = [ring_stack] + [
            lax.ppermute(ring_stack, axes, y_perm(k)) for k in range(1, y_count)
        ]
        y_stack = jnp.stack(y_parts)
        both = jnp.stack([y_stack, lax.ppermute(y_stack, axes, pair_perm)])
        return both.reshape(-1, local.shape[-1])

    kc = jnp.arange(2, dtype=jnp.int32)[:, None, None]
    ky = jnp.arange(y_count, dtype=jnp.int32)[None, :, None]
    kz = jnp.arange(4, dtype=jnp.int32)[None, None, :]
    src_ring = (me_ring - kz) % 4
    actor_of = (
        (src_ring % 2) * cp_count
        + ((me_y - ky) % y_count) * 4
        + (src_ring // 2) * 2
        + (me_core ^ kc)
    ).reshape(blocks)
    half = own_rows // 2
    rows_parts = [gather_rows(rollout_rows[:half]), gather_rows(rollout_rows[half:])]

    block_ids = jnp.arange(blocks, dtype=jnp.int32)
    packed_block = jnp.sum(
        jnp.where(block_owner[None, :] == block_ids[:, None], block_ids[None, :], 0), axis=1
    )
    inner = jnp.arange(own_rows, dtype=jnp.int32)
    half_inner = jnp.arange(half, dtype=jnp.int32)
    layout_start = packed_block[actor_of] * own_rows
    position = jnp.concatenate(
        [
            (layout_start[:, None] + half_inner[None, :]).reshape(-1),
            (layout_start[:, None] + half + half_inner[None, :]).reshape(-1),
        ]
    )
    query_order = (
        packed_block.reshape(sections, y_count, 2, 2).transpose(3, 1, 2, 0).reshape(blocks)
    )
    query_position = (query_order[:, None] * own_rows + inner[None, :]).reshape(tokens)
    seq_ends = jnp.cumsum(lengths)
    sequence = jnp.sum((position[:, None] >= seq_ends[None, :]).astype(jnp.int32), axis=1)
    query_sequence = jnp.sum(
        (query_position[:, None] >= seq_ends[None, :]).astype(jnp.int32), axis=1
    )

    me_tp = lax.axis_index("tp")
    qkv_weights = w_qkv[0]

    def project(rows_in):
        rows_f32 = rows_in.astype(jnp.float32)
        squares = jnp.sum(jnp.square(rows_f32), axis=1)
        total_squares = squares
        for step in range(1, tp_count):
            total_squares = total_squares + shifted(squares, "tp", tp_count, step)
        inverse_rms = lax.rsqrt(total_squares / D + 1e-05)
        scaled = (rows_f32 * norm_gain[0][None, :]).astype(jnp.bfloat16)

        def head_partial(head):
            head_weights = lax.dynamic_slice_in_dim(qkv_weights, head * HEAD, HEAD, axis=2)
            return jnp.einsum(
                "rd,kde->kre", scaled, head_weights, preferred_element_type=jnp.float32
            )

        summed = head_partial(me_tp)
        for step in range(1, tp_count):
            piece = head_partial((me_tp + step) % tp_count).astype(jnp.bfloat16)
            summed = summed + shifted(piece, "tp", tp_count, step).astype(jnp.float32)
        return (summed * inverse_rms[None, :, None]).astype(jnp.bfloat16)

    qkv_parts = [project(part) for part in rows_parts]
    key_rows = jnp.concatenate([part[1] for part in qkv_parts], axis=0)
    value_rows = jnp.concatenate([part[2] for part in qkv_parts], axis=0)
    t_core = jnp.arange(2, dtype=jnp.int32)[:, None, None, None]
    t_y = jnp.arange(y_count, dtype=jnp.int32)[None, :, None, None]
    t_z = jnp.arange(2, dtype=jnp.int32)[None, None, :, None]
    t_s = jnp.arange(sections, dtype=jnp.int32)[None, None, None, :]
    layout_of = (
        ((t_core ^ me_core) * y_count + (me_y - t_y) % y_count) * 4
        + (me_ring - (t_z * 2 + t_s)) % 4
    ).reshape(blocks)
    queries = jnp.concatenate(
        [jnp.take(part[0].reshape(blocks, half, HEAD), layout_of, axis=0) for part in qkv_parts],
        axis=1,
    ).reshape(tokens, HEAD)

    out_weight = w_out[0].reshape(tp_count, HEAD, width_here)
    source_of = (me_tp - jnp.arange(tp_count, dtype=jnp.int32)) % tp_count
    out_weight = jnp.take(out_weight, source_of, axis=0)
    z_flip = [(g, g // cp_count * cp_count + (g % cp_count ^ 2)) for g in range(flat)]
    s_flip = [(g, (g + cp_count) % flat) for g in range(flat)]
    both_flip = [
        (g, (g + cp_count) % flat // cp_count * cp_count + (g % cp_count ^ 2)) for g in range(flat)
    ]
    core_perm = [(c, c ^ 1) for c in range(cp_count)]

    def back_half(chunk_queries, chunk_position, chunk_sequence):
        chunk_rows = chunk_queries.shape[0] // blocks
        allowed = (chunk_sequence[:, None] == sequence[None, :]) & (
            position[None, :] <= chunk_position[:, None]
        )
        scores = jnp.dot(chunk_queries, key_rows.T, preferred_element_type=jnp.float32)
        scores = jnp.where(allowed, scores / math.sqrt(HEAD), -1e30)
        row_peak = jnp.max(scores, axis=1, keepdims=True)
        weights = jnp.where(allowed, jnp.exp(scores - row_peak), 0.0)
        row_total = jnp.sum(weights, axis=1, keepdims=True)
        probabilities = weights.astype(jnp.bfloat16)
        mixed = jnp.dot(probabilities, value_rows, preferred_element_type=jnp.float32)
        attended = (mixed / row_total).astype(jnp.bfloat16)
        parts = [attended] + [
            shifted(attended, "tp", tp_count, step) for step in range(1, tp_count)
        ]
        partial_out = jnp.einsum(
            "kre,kew->rw", jnp.stack(parts), out_weight, preferred_element_type=jnp.float32
        ).astype(jnp.bfloat16)
        staged = partial_out.reshape(2, y_count, 2, sections, chunk_rows, width_here)
        kept = lax.dynamic_index_in_dim(staged, me_core, 0, keepdims=False)
        given = lax.dynamic_index_in_dim(staged, 1 - me_core, 0, keepdims=False)
        chip_sum = kept.astype(jnp.float32) + lax.ppermute(given, "cp", core_perm).astype(
            jnp.float32
        )
        chip_half = chip_sum.astype(jnp.bfloat16)
        y_sum = lax.dynamic_index_in_dim(chip_sum, me_y, 0, keepdims=False)
        for step in range(1, y_count):
            piece = lax.dynamic_index_in_dim(
                chip_half, (me_y + step) % y_count, 0, keepdims=False
            )
            y_perm = [(c, ((c // 4 + step) % y_count) * 4 + c % 4) for c in range(cp_count)]
            y_sum = y_sum + lax.ppermute(piece, "cp", y_perm).astype(jnp.float32)
        y_half = y_sum.astype(jnp.bfloat16)

        def piece_of(z_index, section_index):
            z_part = lax.dynamic_index_in_dim(y_half, z_index, 0, keepdims=False)
            return lax.dynamic_index_in_dim(z_part, section_index, 0, keepdims=False)

        own_part = lax.dynamic_index_in_dim(
            lax.dynamic_index_in_dim(y_sum, me_z, 0, keepdims=False), me_section, 0, keepdims=False
        )
        own_total = own_part + lax.ppermute(piece_of(1 - me_z, me_section), axes, z_flip).astype(
            jnp.float32
        )
        other_total = lax.ppermute(piece_of(me_z, 1 - me_section), axes, s_flip).astype(
            jnp.float32
        ) + lax.ppermute(piece_of(1 - me_z, 1 - me_section), axes, both_flip).astype(jnp.float32)
        return own_total.astype(jnp.bfloat16), other_total.astype(jnp.bfloat16)

    chunks = 4
    chunk_rows = own_rows // chunks
    query_blocks = queries.reshape(blocks, own_rows, HEAD)
    position_blocks = query_position.reshape(blocks, own_rows)
    sequence_blocks = query_sequence.reshape(blocks, own_rows)
    own_parts, other_parts = [], []
    for chunk in range(chunks):
        rows_of = slice(chunk * chunk_rows, (chunk + 1) * chunk_rows)
        own_part, other_part = back_half(
            query_blocks[:, rows_of].reshape(-1, HEAD),
            position_blocks[:, rows_of].reshape(-1),
            sequence_blocks[:, rows_of].reshape(-1),
        )
        own_parts.append(own_part)
        other_parts.append(other_part)
    own_total = jnp.concatenate(own_parts, axis=0)
    other_total = jnp.concatenate(other_parts, axis=0)
    return jnp.where(
        me_section == 0, jnp.stack([own_total, other_total]), jnp.stack([other_total, own_total])
    )

def solution(mesh):
    return jax.shard_map(
        on_device,
        mesh=mesh,
        in_specs=(
            P(("section", "cp"), "tp"),
            P(),
            P(),
            P("section", "tp"),
            P("section", None, "tp", "cp"),
            P("section", "cp", "tp"),
        ),
        out_specs=P(None, ("section", "cp"), "tp"),
        check_vma=False,
    )
```

```python
import math

import jax
import jax.numpy as jnp
from jax import lax
from jax.sharding import PartitionSpec as P

D = 8192
HEAD = 128


def shifted(value, axis, count, step):
    return lax.ppermute(value, axis, perm=[(j, (j + step) % count) for j in range(count)])


def on_device(rollout_rows, lengths, block_owner, norm_gain, w_qkv, w_out):
    tp_count = lax.axis_size("tp")
    cp_count = lax.axis_size("cp")
    sections = lax.axis_size("section")
    own_rows, width_here = rollout_rows.shape
    blocks = sections * cp_count
    tokens = own_rows * blocks

    y_count = cp_count // 4
    me_section = lax.axis_index("section")
    me_cp = lax.axis_index("cp")
    me_core = me_cp % 2
    me_y = me_cp // 4
    me_z = me_cp // 2 % 2
    me_ring = me_z * 2 + me_section
    flat = sections * cp_count
    axes = ("section", "cp")

    def coords(g):
        c = g % cp_count
        return g // cp_count, c // 4, c // 2 % 2, c % 2

    def linear(s_i, y_i, z_i, core_i):
        return s_i * cp_count + y_i * 4 + z_i * 2 + core_i

    def ring_perm(step):
        pairs = []
        for g in range(flat):
            s_i, y_i, z_i, core_i = coords(g)
            ring = (z_i * 2 + s_i + step) % 4
            pairs.append((g, linear(ring % 2, y_i, ring // 2, core_i)))
        return pairs

    def y_perm(step):
        pairs = []
        for g in range(flat):
            s_i, y_i, z_i, core_i = coords(g)
            pairs.append((g, linear(s_i, (y_i + step) % y_count, z_i, core_i)))
        return pairs

    pair_perm = [(g, g ^ 1) for g in range(flat)]

    def gather_rows(local):
        ring_parts = [local] + [lax.ppermute(local, axes, ring_perm(k)) for k in range(1, 4)]
        ring_stack = jnp.stack(ring_parts)
        y_parts = [ring_stack] + [
            lax.ppermute(ring_stack, axes, y_perm(k)) for k in range(1, y_count)
        ]
        y_stack = jnp.stack(y_parts)
        both = jnp.stack([y_stack, lax.ppermute(y_stack, axes, pair_perm)])
        return both.reshape(-1, local.shape[-1])

    kc = jnp.arange(2, dtype=jnp.int32)[:, None, None]
    ky = jnp.arange(y_count, dtype=jnp.int32)[None, :, None]
    kz = jnp.arange(4, dtype=jnp.int32)[None, None, :]
    src_ring = (me_ring - kz) % 4
    actor_of = (
        (src_ring % 2) * cp_count
        + ((me_y - ky) % y_count) * 4
        + (src_ring // 2) * 2
        + (me_core ^ kc)
    ).reshape(blocks)
    half = own_rows // 2
    rows_parts = [gather_rows(rollout_rows[:half]), gather_rows(rollout_rows[half:])]

    block_ids = jnp.arange(blocks, dtype=jnp.int32)
    packed_block = jnp.sum(
        jnp.where(block_owner[None, :] == block_ids[:, None], block_ids[None, :], 0), axis=1
    )
    inner = jnp.arange(own_rows, dtype=jnp.int32)
    half_inner = jnp.arange(half, dtype=jnp.int32)
    layout_start = packed_block[actor_of] * own_rows
    position = jnp.concatenate(
        [
            (layout_start[:, None] + half_inner[None, :]).reshape(-1),
            (layout_start[:, None] + half + half_inner[None, :]).reshape(-1),
        ]
    )
    query_order = (
        packed_block.reshape(sections, y_count, 2, 2).transpose(3, 1, 2, 0).reshape(blocks)
    )
    query_position = (query_order[:, None] * own_rows + inner[None, :]).reshape(tokens)
    seq_ends = jnp.cumsum(lengths)
    sequence = jnp.sum((position[:, None] >= seq_ends[None, :]).astype(jnp.int32), axis=1)
    query_sequence = jnp.sum(
        (query_position[:, None] >= seq_ends[None, :]).astype(jnp.int32), axis=1
    )

    me_tp = lax.axis_index("tp")
    qkv_weights = w_qkv[0]

    def project(rows_in):
        rows_f32 = rows_in.astype(jnp.float32)
        squares = jnp.sum(jnp.square(rows_f32), axis=1)
        total_squares = squares
        for step in range(1, tp_count):
            total_squares = total_squares + shifted(squares, "tp", tp_count, step)
        inverse_rms = lax.rsqrt(total_squares / D + 1e-05)
        scaled = (rows_f32 * norm_gain[0][None, :]).astype(jnp.bfloat16)

        def head_partial(head):
            head_weights = lax.dynamic_slice_in_dim(qkv_weights, head * HEAD, HEAD, axis=2)
            return jnp.einsum(
                "rd,kde->kre", scaled, head_weights, preferred_element_type=jnp.float32
            )

        summed = head_partial(me_tp)
        for step in range(1, tp_count):
            piece = head_partial((me_tp + step) % tp_count).astype(jnp.bfloat16)
            summed = summed + shifted(piece, "tp", tp_count, step).astype(jnp.float32)
        return (summed * inverse_rms[None, :, None]).astype(jnp.bfloat16)

    qkv_parts = [project(part) for part in rows_parts]
    key_rows = jnp.concatenate([part[1] for part in qkv_parts], axis=0)
    value_rows = jnp.concatenate([part[2] for part in qkv_parts], axis=0)
    t_core = jnp.arange(2, dtype=jnp.int32)[:, None, None, None]
    t_y = jnp.arange(y_count, dtype=jnp.int32)[None, :, None, None]
    t_z = jnp.arange(2, dtype=jnp.int32)[None, None, :, None]
    t_s = jnp.arange(sections, dtype=jnp.int32)[None, None, None, :]
    layout_of = (
        ((t_core ^ me_core) * y_count + (me_y - t_y) % y_count) * 4
        + (me_ring - (t_z * 2 + t_s)) % 4
    ).reshape(blocks)
    queries = jnp.concatenate(
        [jnp.take(part[0].reshape(blocks, half, HEAD), layout_of, axis=0) for part in qkv_parts],
        axis=1,
    ).reshape(tokens, HEAD)

    out_weight = w_out[0].reshape(tp_count, HEAD, width_here)
    source_of = (me_tp - jnp.arange(tp_count, dtype=jnp.int32)) % tp_count
    out_weight = jnp.take(out_weight, source_of, axis=0)
    z_flip = [(g, g // cp_count * cp_count + (g % cp_count ^ 2)) for g in range(flat)]
    s_flip = [(g, (g + cp_count) % flat) for g in range(flat)]
    both_flip = [
        (g, (g + cp_count) % flat // cp_count * cp_count + (g % cp_count ^ 2)) for g in range(flat)
    ]
    core_perm = [(c, c ^ 1) for c in range(cp_count)]

    def back_half(chunk_queries, chunk_position, chunk_sequence):
        chunk_rows = chunk_queries.shape[0] // blocks
        allowed = (chunk_sequence[:, None] == sequence[None, :]) & (
            position[None, :] <= chunk_position[:, None]
        )
        scores = jnp.dot(chunk_queries, key_rows.T, preferred_element_type=jnp.float32)
        scores = jnp.where(allowed, scores / math.sqrt(HEAD), -1e30)
        row_peak = jnp.max(scores, axis=1, keepdims=True)
        weights = jnp.where(allowed, jnp.exp(scores - row_peak), 0.0)
        row_total = jnp.sum(weights, axis=1, keepdims=True)
        probabilities = weights.astype(jnp.bfloat16)
        mixed = jnp.dot(probabilities, value_rows, preferred_element_type=jnp.float32)
        attended = (mixed / row_total).astype(jnp.bfloat16)
        parts = [attended] + [
            shifted(attended, "tp", tp_count, step) for step in range(1, tp_count)
        ]
        partial_out = jnp.einsum(
            "kre,kew->rw", jnp.stack(parts), out_weight, preferred_element_type=jnp.float32
        ).astype(jnp.bfloat16)
        staged = partial_out.reshape(2, y_count, 2, sections, chunk_rows, width_here)
        kept = lax.dynamic_index_in_dim(staged, me_core, 0, keepdims=False)
        given = lax.dynamic_index_in_dim(staged, 1 - me_core, 0, keepdims=False)
        arrived = lax.ppermute(given, "cp", core_perm)
        chip_half = (kept.astype(jnp.float32) + arrived.astype(jnp.float32)).astype(jnp.bfloat16)
        y_sum = lax.dynamic_index_in_dim(kept, me_y, 0, keepdims=False).astype(
            jnp.float32
        ) + lax.dynamic_index_in_dim(arrived, me_y, 0, keepdims=False).astype(jnp.float32)
        for step in range(1, y_count):
            piece = lax.dynamic_index_in_dim(
                chip_half, (me_y + step) % y_count, 0, keepdims=False
            )
            y_perm = [(c, ((c // 4 + step) % y_count) * 4 + c % 4) for c in range(cp_count)]
            y_sum = y_sum + lax.ppermute(piece, "cp", y_perm).astype(jnp.float32)
        y_half = y_sum.astype(jnp.bfloat16)

        def piece_of(z_index, section_index):
            z_part = lax.dynamic_index_in_dim(y_half, z_index, 0, keepdims=False)
            return lax.dynamic_index_in_dim(z_part, section_index, 0, keepdims=False)

        own_part = lax.dynamic_index_in_dim(
            lax.dynamic_index_in_dim(y_sum, me_z, 0, keepdims=False), me_section, 0, keepdims=False
        )
        own_total = own_part + lax.ppermute(piece_of(1 - me_z, me_section), axes, z_flip).astype(
            jnp.float32
        )
        other_total = lax.ppermute(piece_of(me_z, 1 - me_section), axes, s_flip).astype(
            jnp.float32
        ) + lax.ppermute(piece_of(1 - me_z, 1 - me_section), axes, both_flip).astype(jnp.float32)
        return own_total.astype(jnp.bfloat16), other_total.astype(jnp.bfloat16)

    chunks = 2
    chunk_rows = own_rows // chunks
    query_blocks = queries.reshape(blocks, own_rows, HEAD)
    position_blocks = query_position.reshape(blocks, own_rows)
    sequence_blocks = query_sequence.reshape(blocks, own_rows)
    own_parts, other_parts = [], []
    for chunk in range(chunks):
        rows_of = slice(chunk * chunk_rows, (chunk + 1) * chunk_rows)
        own_part, other_part = back_half(
            query_blocks[:, rows_of].reshape(-1, HEAD),
            position_blocks[:, rows_of].reshape(-1),
            sequence_blocks[:, rows_of].reshape(-1),
        )
        own_parts.append(own_part)
        other_parts.append(other_part)
    own_total = jnp.concatenate(own_parts, axis=0)
    other_total = jnp.concatenate(other_parts, axis=0)
    return jnp.where(
        me_section == 0, jnp.stack([own_total, other_total]), jnp.stack([other_total, own_total])
    )

def solution(mesh):
    return jax.shard_map(
        on_device,
        mesh=mesh,
        in_specs=(
            P(("section", "cp"), "tp"),
            P(),
            P(),
            P("section", "tp"),
            P("section", None, "tp", "cp"),
            P("section", "cp", "tp"),
        ),
        out_specs=P(None, ("section", "cp"), "tp"),
        check_vma=False,
    )
```

```python
import math

import jax
import jax.numpy as jnp
from jax import lax
from jax.sharding import PartitionSpec as P

D = 8192
HEAD = 128


def shifted(value, axis, count, step):
    return lax.ppermute(value, axis, perm=[(j, (j + step) % count) for j in range(count)])


def on_device(rollout_rows, lengths, block_owner, norm_gain, w_qkv, w_out):
    tp_count = lax.axis_size("tp")
    cp_count = lax.axis_size("cp")
    sections = lax.axis_size("section")
    own_rows, width_here = rollout_rows.shape
    blocks = sections * cp_count
    tokens = own_rows * blocks

    y_count = cp_count // 4
    me_section = lax.axis_index("section")
    me_cp = lax.axis_index("cp")
    me_core = me_cp % 2
    me_y = me_cp // 4
    me_z = me_cp // 2 % 2
    me_ring = me_z * 2 + me_section
    flat = sections * cp_count
    axes = ("section", "cp")

    def coords(g):
        c = g % cp_count
        return g // cp_count, c // 4, c // 2 % 2, c % 2

    def linear(s_i, y_i, z_i, core_i):
        return s_i * cp_count + y_i * 4 + z_i * 2 + core_i

    def ring_perm(step):
        pairs = []
        for g in range(flat):
            s_i, y_i, z_i, core_i = coords(g)
            ring = (z_i * 2 + s_i + step) % 4
            pairs.append((g, linear(ring % 2, y_i, ring // 2, core_i)))
        return pairs

    def y_perm(step):
        pairs = []
        for g in range(flat):
            s_i, y_i, z_i, core_i = coords(g)
            pairs.append((g, linear(s_i, (y_i + step) % y_count, z_i, core_i)))
        return pairs

    pair_perm = [(g, g ^ 1) for g in range(flat)]

    def gather_rows(local):
        ring_parts = [local] + [lax.ppermute(local, axes, ring_perm(k)) for k in range(1, 4)]
        ring_stack = jnp.stack(ring_parts)
        y_parts = [ring_stack] + [
            lax.ppermute(ring_stack, axes, y_perm(k)) for k in range(1, y_count)
        ]
        y_stack = jnp.stack(y_parts)
        both = jnp.stack([y_stack, lax.ppermute(y_stack, axes, pair_perm)])
        return both.reshape(-1, local.shape[-1])

    kc = jnp.arange(2, dtype=jnp.int32)[:, None, None]
    ky = jnp.arange(y_count, dtype=jnp.int32)[None, :, None]
    kz = jnp.arange(4, dtype=jnp.int32)[None, None, :]
    src_ring = (me_ring - kz) % 4
    actor_of = (
        (src_ring % 2) * cp_count
        + ((me_y - ky) % y_count) * 4
        + (src_ring // 2) * 2
        + (me_core ^ kc)
    ).reshape(blocks)
    half = own_rows // 2
    rows_parts = [gather_rows(rollout_rows[:half]), gather_rows(rollout_rows[half:])]

    block_ids = jnp.arange(blocks, dtype=jnp.int32)
    packed_block = jnp.sum(
        jnp.where(block_owner[None, :] == block_ids[:, None], block_ids[None, :], 0), axis=1
    )
    inner = jnp.arange(own_rows, dtype=jnp.int32)
    half_inner = jnp.arange(half, dtype=jnp.int32)
    layout_start = packed_block[actor_of] * own_rows
    position = jnp.concatenate(
        [
            (layout_start[:, None] + half_inner[None, :]).reshape(-1),
            (layout_start[:, None] + half + half_inner[None, :]).reshape(-1),
        ]
    )
    query_order = (
        packed_block.reshape(sections, y_count, 2, 2).transpose(3, 1, 2, 0).reshape(blocks)
    )
    query_position = (query_order[:, None] * own_rows + inner[None, :]).reshape(tokens)
    seq_ends = jnp.cumsum(lengths)
    sequence = jnp.sum((position[:, None] >= seq_ends[None, :]).astype(jnp.int32), axis=1)
    query_sequence = jnp.sum(
        (query_position[:, None] >= seq_ends[None, :]).astype(jnp.int32), axis=1
    )

    me_tp = lax.axis_index("tp")
    qkv_weights = w_qkv[0]

    def project(rows_in):
        rows_f32 = rows_in.astype(jnp.float32)
        squares = jnp.sum(jnp.square(rows_f32), axis=1)
        total_squares = squares
        for step in range(1, tp_count):
            total_squares = total_squares + shifted(squares, "tp", tp_count, step)
        inverse_rms = lax.rsqrt(total_squares / D + 1e-05)
        scaled = (rows_f32 * norm_gain[0][None, :]).astype(jnp.bfloat16)

        def head_partial(head):
            head_weights = lax.dynamic_slice_in_dim(qkv_weights, head * HEAD, HEAD, axis=2)
            return jnp.einsum(
                "rd,kde->kre", scaled, head_weights, preferred_element_type=jnp.float32
            )

        summed = head_partial(me_tp)
        far = tp_count // 2
        for step in [far] + [k for k in range(1, tp_count) if k != far]:
            piece = head_partial((me_tp + step) % tp_count).astype(jnp.bfloat16)
            summed = summed + shifted(piece, "tp", tp_count, step).astype(jnp.float32)
        return (summed * inverse_rms[None, :, None]).astype(jnp.bfloat16)

    qkv_parts = [project(part) for part in rows_parts]
    key_rows = jnp.concatenate([part[1] for part in qkv_parts], axis=0)
    value_rows = jnp.concatenate([part[2] for part in qkv_parts], axis=0)
    t_core = jnp.arange(2, dtype=jnp.int32)[:, None, None, None]
    t_y = jnp.arange(y_count, dtype=jnp.int32)[None, :, None, None]
    t_z = jnp.arange(2, dtype=jnp.int32)[None, None, :, None]
    t_s = jnp.arange(sections, dtype=jnp.int32)[None, None, None, :]
    layout_of = (
        ((t_core ^ me_core) * y_count + (me_y - t_y) % y_count) * 4
        + (me_ring - (t_z * 2 + t_s)) % 4
    ).reshape(blocks)
    queries = jnp.concatenate(
        [jnp.take(part[0].reshape(blocks, half, HEAD), layout_of, axis=0) for part in qkv_parts],
        axis=1,
    ).reshape(tokens, HEAD)

    out_weight = w_out[0].reshape(tp_count, HEAD, width_here)
    source_of = (me_tp - jnp.arange(tp_count, dtype=jnp.int32)) % tp_count
    out_weight = jnp.take(out_weight, source_of, axis=0)
    z_flip = [(g, g // cp_count * cp_count + (g % cp_count ^ 2)) for g in range(flat)]
    s_flip = [(g, (g + cp_count) % flat) for g in range(flat)]
    both_flip = [
        (g, (g + cp_count) % flat // cp_count * cp_count + (g % cp_count ^ 2)) for g in range(flat)
    ]
    core_perm = [(c, c ^ 1) for c in range(cp_count)]

    def back_half(chunk_queries, chunk_position, chunk_sequence):
        chunk_rows = chunk_queries.shape[0] // blocks
        allowed = (chunk_sequence[:, None] == sequence[None, :]) & (
            position[None, :] <= chunk_position[:, None]
        )
        scores = jnp.dot(chunk_queries, key_rows.T, preferred_element_type=jnp.float32)
        scores = jnp.where(allowed, scores / math.sqrt(HEAD), -1e30)
        row_peak = jnp.max(scores, axis=1, keepdims=True)
        weights = jnp.where(allowed, jnp.exp(scores - row_peak), 0.0)
        row_total = jnp.sum(weights, axis=1, keepdims=True)
        probabilities = weights.astype(jnp.bfloat16)
        mixed = jnp.dot(probabilities, value_rows, preferred_element_type=jnp.float32)
        attended = (mixed / row_total).astype(jnp.bfloat16)
        parts = [attended] + [
            shifted(attended, "tp", tp_count, step) for step in range(1, tp_count)
        ]
        partial_out = jnp.einsum(
            "kre,kew->rw", jnp.stack(parts), out_weight, preferred_element_type=jnp.float32
        ).astype(jnp.bfloat16)
        staged = partial_out.reshape(2, y_count, 2, sections, chunk_rows, width_here)
        kept = lax.dynamic_index_in_dim(staged, me_core, 0, keepdims=False)
        given = lax.dynamic_index_in_dim(staged, 1 - me_core, 0, keepdims=False)
        chip_sum = kept.astype(jnp.float32) + lax.ppermute(given, "cp", core_perm).astype(
            jnp.float32
        )
        chip_half = chip_sum.astype(jnp.bfloat16)
        y_sum = lax.dynamic_index_in_dim(chip_sum, me_y, 0, keepdims=False)
        for step in range(1, y_count):
            piece = lax.dynamic_index_in_dim(
                chip_half, (me_y + step) % y_count, 0, keepdims=False
            )
            y_perm = [(c, ((c // 4 + step) % y_count) * 4 + c % 4) for c in range(cp_count)]
            y_sum = y_sum + lax.ppermute(piece, "cp", y_perm).astype(jnp.float32)
        y_half = y_sum.astype(jnp.bfloat16)

        def piece_of(z_index, section_index):
            z_part = lax.dynamic_index_in_dim(y_half, z_index, 0, keepdims=False)
            return lax.dynamic_index_in_dim(z_part, section_index, 0, keepdims=False)

        own_part = lax.dynamic_index_in_dim(
            lax.dynamic_index_in_dim(y_sum, me_z, 0, keepdims=False), me_section, 0, keepdims=False
        )
        own_total = own_part + lax.ppermute(piece_of(1 - me_z, me_section), axes, z_flip).astype(
            jnp.float32
        )
        other_total = lax.ppermute(piece_of(me_z, 1 - me_section), axes, s_flip).astype(
            jnp.float32
        ) + lax.ppermute(piece_of(1 - me_z, 1 - me_section), axes, both_flip).astype(jnp.float32)
        return own_total.astype(jnp.bfloat16), other_total.astype(jnp.bfloat16)

    chunks = 2
    chunk_rows = own_rows // chunks
    query_blocks = queries.reshape(blocks, own_rows, HEAD)
    position_blocks = query_position.reshape(blocks, own_rows)
    sequence_blocks = query_sequence.reshape(blocks, own_rows)
    own_parts, other_parts = [], []
    for chunk in range(chunks):
        rows_of = slice(chunk * chunk_rows, (chunk + 1) * chunk_rows)
        own_part, other_part = back_half(
            query_blocks[:, rows_of].reshape(-1, HEAD),
            position_blocks[:, rows_of].reshape(-1),
            sequence_blocks[:, rows_of].reshape(-1),
        )
        own_parts.append(own_part)
        other_parts.append(other_part)
    own_total = jnp.concatenate(own_parts, axis=0)
    other_total = jnp.concatenate(other_parts, axis=0)
    return jnp.where(
        me_section == 0, jnp.stack([own_total, other_total]), jnp.stack([other_total, own_total])
    )

def solution(mesh):
    return jax.shard_map(
        on_device,
        mesh=mesh,
        in_specs=(
            P(("section", "cp"), "tp"),
            P(),
            P(),
            P("section", "tp"),
            P("section", None, "tp", "cp"),
            P("section", "cp", "tp"),
        ),
        out_specs=P(None, ("section", "cp"), "tp"),
        check_vma=False,
    )
```
